512 devices in a mesh: dp: 16 (over x, z_lo, core), seq: 32 (over z_hi, y).
Axes of the slice: x: 4, y: 8, z: 8 (z_hi: 4, z_lo: 2; z = z_hi * 2 + z_lo), core: 2. Of those that a mesh axis runs over, the one named last changes fastest.
Arguments:
- ssm_input: bfloat16 [16, 8192, 1024], P('dp', 'seq'), may hold values from -6 to 6
- gate_input: bfloat16 [16, 8192, 1024], P('dp', 'seq'), may hold values from -6 to 6
- state_proj: bfloat16 [16, 8192, 512], P('dp', 'seq'), may hold values from -6 to 6
- step_raw: float32 [16, 32, 8192], P('dp', None, 'seq'), may hold values from -5 to 400
- decay_log: float32 [2, 16], replicated, may hold values from -10 to 0
- skip_gain: float32 [16], replicated, may hold values from 0.5 to 2
- norm_gain: float32 [1024], replicated, may hold values from 0.25 to 1.75
- out_weight: bfloat16 [1024, 1024], P('dp'), may hold values from -0.1875 to 0.1875
- latents: bfloat16 [256, 1024], replicated, may hold values from -450 to 450
- lengths: int32 [16], P('dp'), may hold values from 4096 to 8192, as said below
Outputs:
- encoded: bfloat16 [16, 8192, 1024], P('dp', 'seq')
- pooled: bfloat16 [16, 256, 1024], P('dp')
The draws below stay inside these ranges and needn't reach their ends.
Inputs may be any that keep to these rules, and one draw needn't show every extreme that they name: `lengths`: positions at or after a sequence's length are padding; at least one sequence has none, and one has 4096 real tokens.
All inputs are finite; a program needn't handle non-finite values.
Results may differ from the reference program's by a relative error of at most 0.034.
Values may be sent and summed in bfloat16 or wider, within the bound.
No kernel may reach another device: no remote copies, remote signals or barrier semaphores. Data moves between devices by JAX's collectives and lax.ppermute only.
A program may use at most 128 MiB of HBM per device.

```python
import math
import jax
import jax.numpy as jnp
from jax import lax

D = 1024
MIXER_HEADS = 16
P_SIZE = 64
STATE = 128
BLOCK = 128
R = 256
L_DEV = 256
HP = 1024
SEQUENCE_TOKENS = 8192
SEQUENCE_COUNT = 16


spike_total = 3


def common_lookup_tables(key):
    base_key = jax.random.fold_in(key, 4711)
    random_key_list = jax.random.split(base_key, 6)
    fast_chance = 0.5
    is_fast = jax.random.bernoulli(random_key_list[0], fast_chance, (2, MIXER_HEADS))
    slow_rate = 20.0 * jnp.exp(jax.random.uniform(random_key_list[1], (2, MIXER_HEADS), minval=math.log(0.3), maxval=0.0)) / SEQUENCE_TOKENS
    fast_rate = jnp.exp(jax.random.uniform(random_key_list[2], (2, MIXER_HEADS), minval=math.log(0.4), maxval=math.log(0.67)))
    forget_rate = jnp.where(is_fast, fast_rate, slow_rate)
    jolt_placement_slot = jax.random.randint(random_key_list[3], (SEQUENCE_COUNT, spike_total), 0, SEQUENCE_TOKENS)
    spike_loss = jax.random.uniform(random_key_list[4], (SEQUENCE_COUNT, 2 * MIXER_HEADS, spike_total), minval=0.2, maxval=0.45)
    return (forget_rate, jolt_placement_slot, spike_loss, random_key_list[5])


def draw_decay_log(key, part):
    forget_rate, unused_item, unused_item, unused_item = common_lookup_tables(key)
    return jnp.log(forget_rate)


def draw_step_raw(key, part):
    forget_rate, jolt_placement_slot, spike_loss, reserve_random_key = common_lookup_tables(key)
    first_key, second_key = jax.random.split(reserve_random_key)
    typical = jnp.exp(jax.random.uniform(first_key, (SEQUENCE_COUNT, 2 * MIXER_HEADS, SEQUENCE_TOKENS), minval=math.log(0.02), maxval=math.log(0.1)))
    factor = jnp.exp(jax.random.uniform(second_key, (SEQUENCE_COUNT, 2 * MIXER_HEADS, SEQUENCE_TOKENS // L_DEV), minval=math.log(0.5), maxval=math.log(2.0)))
    quantized_stride_width = typical * jnp.repeat(factor, L_DEV, axis=2)
    jolt_stride_amount = jnp.minimum(spike_loss / forget_rate.reshape(2 * MIXER_HEADS)[None, :, None], 400.0)
    symbol_offset = jnp.arange(SEQUENCE_TOKENS, dtype=jnp.int32)
    for jolt_ordinal in range(spike_total):
        within_outburst_range = symbol_offset[None, None, :] == jolt_placement_slot[:, jolt_ordinal][:, None, None]
        quantized_stride_width = jnp.where(within_outburst_range, jnp.maximum(quantized_stride_width, jolt_stride_amount[:, :, jolt_ordinal][:, :, None]), quantized_stride_width)
    return quantized_stride_width + jnp.log(-jnp.expm1(-quantized_stride_width))


def draw_state_proj(key, part):
    unused_item, jolt_placement_slot, unused_item, unused_item = common_lookup_tables(key)
    values = jnp.clip(jax.random.normal(jax.random.fold_in(key, 77), (SEQUENCE_COUNT, SEQUENCE_TOKENS, 4 * STATE)), -6.0, 6.0)
    symbol_offset = jnp.arange(SEQUENCE_TOKENS, dtype=jnp.int32)
    within_outburst_range = jnp.any(symbol_offset[None, None, :] == jolt_placement_slot[:, :, None], axis=1)
    column = jnp.arange(4 * STATE, dtype=jnp.int32)
    entering_mapping_vector = (column < STATE) | (column >= 2 * STATE) & (column < 3 * STATE)
    contraction_multiplier = jnp.where(within_outburst_range[:, :, None] & entering_mapping_vector[None, None, :], 0.01, 1.0)
    return (values * contraction_multiplier).astype(jnp.bfloat16)


def draw_latents(key, part):
    first_key = jax.random.fold_in(jax.random.fold_in(key, 31), 0)
    values = 2.5 * jnp.clip(jax.random.normal(first_key, (R, D)), -6.0, 6.0)
    return values.astype(jnp.bfloat16)


def draw_lengths(key, part):
    first_key, second_key = jax.random.split(jax.random.fold_in(key, 99))
    counts = jax.random.randint(first_key, (SEQUENCE_COUNT,), SEQUENCE_TOKENS // 2, SEQUENCE_TOKENS + 1)
    shuffled = jax.random.permutation(second_key, SEQUENCE_COUNT)
    counts = counts.at[shuffled[0]].set(SEQUENCE_TOKENS)
    counts = counts.at[shuffled[1]].set(SEQUENCE_TOKENS // 2)
    return counts.astype(jnp.int32)


def level_of(rng, dims, shards, low, top_value):
    loudness = 1.0
    for position, blocks in shards:
        draws = jax.random.uniform(jax.random.fold_in(jax.random.fold_in(rng, 6), position), (blocks,), jnp.float32, low / len(shards), top_value / len(shards))
        loudness = loudness * jnp.repeat(jnp.exp(draws), dims[position] // blocks).reshape((-1,) + (1,) * (len(dims) - 1 - position))
    return loudness


def normal_values(rng, dims, scale, limit, shards=(), held_as=jnp.bfloat16):
    values = jax.random.normal(rng, dims, jnp.float32) * scale
    if len(shards) > 0:
        values = level_of(rng, dims, shards, -0.22, 0.18) * values
    return jnp.clip(values, min=-limit, max=limit).astype(held_as)


def setup_inputs(seed: int = 0) -> dict:
    splits = jax.random.split(jax.random.key(seed), 11)
    ssm_input = normal_values(splits[0], (SEQUENCE_COUNT, SEQUENCE_TOKENS, HP), 1.0, 6.0, ((0, 16), (1, 32)))
    gate_input = normal_values(splits[1], (SEQUENCE_COUNT, SEQUENCE_TOKENS, HP), 1.0, 6.0, ((0, 16), (1, 32)))
    state_proj = draw_state_proj(jax.random.fold_in(splits[10], 71), 0)
    step_raw = draw_step_raw(jax.random.fold_in(splits[10], 71), 0)
    decay_log = draw_decay_log(jax.random.fold_in(splits[10], 71), 0)
    skip_gain = jnp.clip(jax.random.uniform(splits[5], (MIXER_HEADS,), jnp.float32, 0.5, 2.0), 0.5, 2.0)
    norm_gain = jnp.clip(1.0 + 0.15 * jax.random.normal(splits[6], (HP,), jnp.float32), 0.25, 1.75)
    out_weight = normal_values(splits[7], (HP, D), HP ** -0.5, 0.1875, ((0, 16),))
    latents = draw_latents(jax.random.fold_in(splits[10], 71), 0)
    lengths = draw_lengths(jax.random.fold_in(splits[10], 71), 0)
    return {"ssm_input": ssm_input, "gate_input": gate_input, "state_proj": state_proj, "step_raw": step_raw, "decay_log": decay_log, "skip_gain": skip_gain, "norm_gain": norm_gain, "out_weight": out_weight, "latents": latents, "lengths": lengths}


def block_terms(x_block, dt_block, b_block, c_block, forget_rate):
    cumulative = jnp.cumsum(-dt_block * forget_rate[:, None], axis=1)
    gram_matrix = jnp.dot(c_block, b_block.T, preferred_element_type=jnp.float32)
    symbol_offset = jnp.arange(x_block.shape[0], dtype=jnp.int32)
    causal = symbol_offset[:, None] >= symbol_offset[None, :]
    spread = jnp.where(causal[None], cumulative[:, :, None] - cumulative[:, None, :], -jnp.inf)
    mixing = (gram_matrix[None] * jnp.exp(spread) * dt_block[:, None, :]).astype(jnp.bfloat16)
    mixing = lax.optimization_barrier(mixing)
    intra_out = jnp.einsum('hqk,khp->qhp', mixing.astype(jnp.float32), x_block.astype(jnp.float32))
    tail_weight = jnp.exp(cumulative[:, -1:] - cumulative) * dt_block
    scaled_x = (x_block.astype(jnp.float32) * tail_weight.T[:, :, None]).astype(jnp.bfloat16)
    scaled_x = lax.optimization_barrier(scaled_x)
    contrib = jnp.einsum('khp,kn->hpn', scaled_x.astype(jnp.float32), b_block.astype(jnp.float32))
    return (intra_out, cumulative, contrib)

def scan_sequence(x_seq, dt_seq, b_seq, c_seq, forget_rate):
    block_count = x_seq.shape[0] // BLOCK
    x_blocks = x_seq.reshape(block_count, BLOCK, MIXER_HEADS, P_SIZE)
    dt_blocks = dt_seq.reshape(MIXER_HEADS, block_count, BLOCK).transpose(1, 0, 2)
    b_blocks = b_seq.reshape(block_count, BLOCK, STATE)
    c_blocks = c_seq.reshape(block_count, BLOCK, STATE)

    def block_step(carried, inputs):
        x_block, dt_block, b_block, c_block = inputs
        intra_out, cumulative, contrib = block_terms(x_block, dt_block, b_block, c_block, forget_rate)
        held_state = lax.optimization_barrier(carried.astype(jnp.bfloat16))
        state_out = jnp.einsum('qn,hpn->qhp', c_block.astype(jnp.float32), held_state.astype(jnp.float32))
        result = intra_out + state_out * jnp.exp(cumulative).T[:, :, None]
        carried = jnp.exp(cumulative[:, -1])[:, None, None] * carried + contrib
        return (carried, result)
    initial = jnp.zeros((MIXER_HEADS, P_SIZE, STATE), jnp.float32)
    unused_item, outputs = lax.scan(block_step, initial, (x_blocks, dt_blocks, b_blocks, c_blocks))
    return outputs.reshape(x_seq.shape[0], MIXER_HEADS, P_SIZE)

def reference(ssm_input, gate_input, state_proj, step_raw, decay_log, skip_gain, norm_gain, out_weight, latents, lengths):
    decay_rates = jnp.exp(decay_log)
    score_scale = 1.0 / math.sqrt(D)
    gain_heads = norm_gain.reshape(MIXER_HEADS, P_SIZE)

    def one_sequence(operands):
        ssm_seq, gate_seq, proj_seq, raw_seq, length = operands
        symbol_offset = jnp.arange(SEQUENCE_TOKENS, dtype=jnp.int32)
        is_valid = symbol_offset < length
        quantized_stride_width = jnp.where(is_valid[None, :], jax.nn.softplus(raw_seq), 0.0)
        tokens = ssm_seq.reshape(SEQUENCE_TOKENS, MIXER_HEADS, P_SIZE)
        forward_out = scan_sequence(tokens, quantized_stride_width[:MIXER_HEADS], proj_seq[:, :STATE], proj_seq[:, STATE:2 * STATE], decay_rates[0])
        backward_out = scan_sequence(tokens[::-1], quantized_stride_width[MIXER_HEADS:, ::-1], proj_seq[::-1, 2 * STATE:3 * STATE], proj_seq[::-1, 3 * STATE:], decay_rates[1])[::-1]
        mixed_out = forward_out + backward_out + skip_gain[None, :, None] * tokens.astype(jnp.float32)
        gated_out = mixed_out * jax.nn.silu(gate_seq.reshape(SEQUENCE_TOKENS, MIXER_HEADS, P_SIZE).astype(jnp.float32))
        mean_square = lax.optimization_barrier(jnp.mean(gated_out * gated_out, axis=2, keepdims=True))
        normed = (gated_out * lax.rsqrt(mean_square + 1e-05) * gain_heads[None]).astype(jnp.bfloat16).reshape(SEQUENCE_TOKENS, HP)
        encoded = jnp.dot(normed, out_weight, preferred_element_type=jnp.float32).astype(jnp.bfloat16)
        scores = jnp.dot(latents, encoded.T, preferred_element_type=jnp.float32) * score_scale
        top_score = lax.optimization_barrier(jnp.max(jnp.where(is_valid[None, :], scores, -1e+30), axis=1))
        prob_values = jnp.where(is_valid[None, :], jnp.exp(scores - top_score[:, None]), 0.0)
        weight_sum = lax.optimization_barrier(jnp.sum(prob_values, axis=1))
        weighted_sum = jnp.dot(prob_values.astype(jnp.bfloat16), encoded, preferred_element_type=jnp.float32)
        pooled = (weighted_sum / weight_sum[:, None]).astype(jnp.bfloat16)
        return (encoded, pooled)
    encoded, pooled = lax.map(one_sequence, (ssm_input, gate_input, state_proj, step_raw, lengths))
    return (encoded, pooled)
```

```python
import math

import jax
import jax.numpy as jnp
from jax import lax
from jax.sharding import PartitionSpec as P

BLOCK = 128


def chain_combine(earlier, later):
    return (
        earlier[0] + later[0],
        jnp.exp(later[0])[:, None, None] * earlier[1] + later[1],
    )


def exclusive_scan(part, axis, reverse):
    count = lax.axis_size(axis)
    inclusive = part
    exclusive = jax.tree.map(jnp.zeros_like, part)
    rounds = max(1, (count - 1).bit_length())
    for k in range(rounds):
        shift = 1 << k
        if shift >= count:
            break
        if reverse:
            perm = [(q, q - shift) for q in range(shift, count)]
        else:
            perm = [(q, q + shift) for q in range(count - shift)]
        received = lax.ppermute(inclusive, axis, perm)
        exclusive = chain_combine(received, exclusive)
        if k + 1 < rounds:
            inclusive = chain_combine(received, inclusive)
    return exclusive


def block_pass(x_seq, dt_seq, b_seq, c_seq, forget_rate):
    row_count, head_count, head_size = x_seq.shape
    state_size = b_seq.shape[1]
    block_count = row_count // BLOCK
    x_blocks = x_seq.reshape(block_count, BLOCK, head_count, head_size)
    dt_blocks = dt_seq.reshape(head_count, block_count, BLOCK).transpose(1, 0, 2)
    b_blocks = b_seq.reshape(block_count, BLOCK, state_size)
    c_blocks = c_seq.reshape(block_count, BLOCK, state_size)
    cumulative = jnp.cumsum(-dt_blocks * forget_rate[None, :, None], axis=2)
    gram_matrix = jnp.einsum(
        "cqn,ckn->cqk", c_blocks, b_blocks, preferred_element_type=jnp.float32
    )
    symbol_offset = jnp.arange(BLOCK, dtype=jnp.int32)
    causal = symbol_offset[:, None] >= symbol_offset[None, :]
    spread = jnp.where(
        causal[None, None], cumulative[:, :, :, None] - cumulative[:, :, None, :], -jnp.inf
    )
    mixing = (gram_matrix[:, None] * jnp.exp(spread) * dt_blocks[:, :, None, :]).astype(
        jnp.bfloat16
    )
    intra_out = jnp.einsum(
        "chqk,ckhp->cqhp", mixing, x_blocks, preferred_element_type=jnp.float32
    )
    block_end = cumulative[:, :, -1]
    tail_weight = jnp.exp(block_end[:, :, None] - cumulative) * dt_blocks
    scaled_x = (x_blocks * tail_weight.transpose(0, 2, 1)[:, :, :, None]).astype(jnp.bfloat16)
    contrib = jnp.einsum(
        "ckhp,ckn->chpn", scaled_x, b_blocks, preferred_element_type=jnp.float32
    )
    decay_sum = jnp.zeros((head_count,), jnp.float32)
    running = jnp.zeros((head_count, head_size, state_size), jnp.float32)
    decay_sums = []
    runnings = []
    for c in range(block_count):
        decay_sums.append(decay_sum)
        runnings.append(running)
        running = jnp.exp(block_end[c])[:, None, None] * running + contrib[c]
        decay_sum = decay_sum + block_end[c]
    records = (intra_out, cumulative, jnp.stack(decay_sums), jnp.stack(runnings), c_blocks)
    return ((decay_sum, running), records)


def apply_state(records, incoming):
    intra_out, cumulative, decay_sums, runnings, c_blocks = records
    block_count = intra_out.shape[0]
    held_state = (
        jnp.exp(decay_sums)[:, :, None, None] * incoming[None] + runnings
    ).astype(jnp.bfloat16)
    state_out = jnp.einsum(
        "cqn,chpn->cqhp", c_blocks, held_state, preferred_element_type=jnp.float32
    )
    outputs = intra_out + state_out * jnp.exp(cumulative).transpose(0, 2, 1)[:, :, :, None]
    return outputs.reshape(block_count * BLOCK, outputs.shape[2] * outputs.shape[3])


def pool_combine(lo, hi):
    top = jnp.maximum(lo[0], hi[0])
    lo_scale = jnp.exp(lo[0] - top)
    hi_scale = jnp.exp(hi[0] - top)
    total = lo[1] * lo_scale + hi[1] * hi_scale
    summed = lo[2] * lo_scale[:, None] + hi[2] * hi_scale[:, None]
    return (top, total, summed)


def butterfly_pool(local, axis):
    count = lax.axis_size(axis)
    assert count & (count - 1) == 0
    place = lax.axis_index(axis)
    state = local
    bit = 1
    while bit < count:
        sent = (state[0], state[1], state[2].astype(jnp.bfloat16))
        perm = [(q, q ^ bit) for q in range(count)]
        received = lax.ppermute(sent, axis, perm)
        own = (sent[0], sent[1], sent[2].astype(jnp.float32))
        other = (received[0], received[1], received[2].astype(jnp.float32))
        is_low = (place & bit) == 0
        lo = jax.tree.map(lambda a, b: jnp.where(is_low, a, b), own, other)
        hi = jax.tree.map(lambda a, b: jnp.where(is_low, b, a), own, other)
        state = pool_combine(lo, hi)
        bit *= 2
    return state


def body(
    ssm_input,
    gate_input,
    state_proj,
    step_raw,
    decay_log,
    skip_gain,
    norm_gain,
    out_weight,
    latents,
    lengths,
):
    row_count = ssm_input.shape[1]
    inner_width = ssm_input.shape[2]
    head_count = decay_log.shape[1]
    head_size = inner_width // head_count
    state_size = state_proj.shape[2] // 4
    model_width = out_weight.shape[1]
    positions = lax.axis_index("seq") * row_count + jnp.arange(row_count, dtype=jnp.int32)
    is_valid = positions < lengths[0]
    step_size = jnp.where(is_valid[None, :], jax.nn.softplus(step_raw[0]), 0.0)
    decay_rates = jnp.exp(decay_log)
    flat_tokens = ssm_input[0]
    tokens = flat_tokens.reshape(row_count, head_count, head_size)
    projections = state_proj[0]
    forward_totals, forward_records = block_pass(
        tokens,
        step_size[:head_count],
        projections[:, :state_size],
        projections[:, state_size : 2 * state_size],
        decay_rates[0],
    )
    backward_totals, backward_records = block_pass(
        tokens[::-1],
        step_size[head_count:, ::-1],
        projections[::-1, 2 * state_size : 3 * state_size],
        projections[::-1, 3 * state_size :],
        decay_rates[1],
    )
    unused_item, forward_in = exclusive_scan(forward_totals, "seq", False)
    unused_item, backward_in = exclusive_scan(backward_totals, "seq", True)
    forward_out = apply_state(forward_records, forward_in)
    backward_out = apply_state(backward_records, backward_in)[::-1]
    skip_wide = jnp.repeat(skip_gain, head_size)
    mixed_out = forward_out + backward_out + skip_wide[None, :] * flat_tokens.astype(jnp.float32)
    gated_out = mixed_out * jax.nn.silu(gate_input[0].astype(jnp.float32))
    squared = (gated_out * gated_out).reshape(row_count, head_count, head_size)
    mean_square = jnp.mean(squared, axis=2)
    inverse_scale = jnp.repeat(lax.rsqrt(mean_square + 1e-05), head_size, axis=1)
    normed = (gated_out * inverse_scale * norm_gain[None, :]).astype(jnp.bfloat16)
    projected = jnp.dot(
        normed,
        lax.all_gather(out_weight, "dp", axis=0, tiled=True),
        preferred_element_type=jnp.float32,
    )
    encoded = projected.astype(jnp.bfloat16)
    score_scale = 1.0 / math.sqrt(model_width)
    scores = (
        jnp.einsum("rd,sd->rs", latents, encoded, preferred_element_type=jnp.float32) * score_scale
    )
    local_top = jnp.max(jnp.where(is_valid[None, :], scores, -1e30), axis=1)
    prob_values = jnp.where(is_valid[None, :], jnp.exp(scores - local_top[:, None]), 0.0)
    weight_sum = jnp.sum(prob_values, axis=1)
    weighted_sum = jnp.dot(
        prob_values.astype(jnp.bfloat16), encoded, preferred_element_type=jnp.float32
    )
    unused_item, total_weight, total_sum = butterfly_pool(
        (local_top, weight_sum, weighted_sum), "seq"
    )
    pooled = (total_sum / total_weight[:, None]).astype(jnp.bfloat16)
    return (encoded[None], pooled[None])


def solution(mesh):
    in_specs = (
        P("dp", "seq", None),
        P("dp", "seq", None),
        P("dp", "seq", None),
        P("dp", None, "seq"),
        P(),
        P(),
        P(),
        P("dp", None),
        P(),
        P("dp"),
    )
    out_specs = (P("dp", "seq", None), P("dp", None, None))
    return jax.shard_map(body, mesh=mesh, in_specs=in_specs, out_specs=out_specs, check_vma=False)
```

```python
import math

import jax
import jax.numpy as jnp
from jax import lax
from jax.sharding import PartitionSpec as P

BLOCK = 128


def chain_combine(earlier, later):
    return (
        earlier[0] + later[0],
        jnp.exp(later[0])[:, None, None] * earlier[1] + later[1],
    )


def exclusive_scan(part, axis, reverse):
    count = lax.axis_size(axis)
    inclusive = part
    exclusive = jax.tree.map(jnp.zeros_like, part)
    rounds = max(1, (count - 1).bit_length())
    for k in range(rounds):
        shift = 1 << k
        if shift >= count:
            break
        if reverse:
            perm = [(q, q - shift) for q in range(shift, count)]
        else:
            perm = [(q, q + shift) for q in range(count - shift)]
        sent = (inclusive[0], inclusive[1].astype(jnp.bfloat16))
        received = lax.ppermute(sent, axis, perm)
        received = (received[0], received[1].astype(jnp.float32))
        exclusive = chain_combine(received, exclusive)
        if k + 1 < rounds:
            inclusive = chain_combine(received, inclusive)
    return exclusive


def block_pass(x_seq, dt_seq, b_seq, c_seq, forget_rate):
    row_count, head_count, head_size = x_seq.shape
    state_size = b_seq.shape[1]
    block_count = row_count // BLOCK
    x_blocks = x_seq.reshape(block_count, BLOCK, head_count, head_size)
    dt_blocks = dt_seq.reshape(head_count, block_count, BLOCK).transpose(1, 0, 2)
    b_blocks = b_seq.reshape(block_count, BLOCK, state_size)
    c_blocks = c_seq.reshape(block_count, BLOCK, state_size)
    cumulative = jnp.cumsum(-dt_blocks * forget_rate[None, :, None], axis=2)
    gram_matrix = jnp.einsum(
        "cqn,ckn->cqk", c_blocks, b_blocks, preferred_element_type=jnp.float32
    )
    symbol_offset = jnp.arange(BLOCK, dtype=jnp.int32)
    causal = symbol_offset[:, None] >= symbol_offset[None, :]
    spread = jnp.where(
        causal[None, None], cumulative[:, :, :, None] - cumulative[:, :, None, :], -jnp.inf
    )
    mixing = (gram_matrix[:, None] * jnp.exp(spread) * dt_blocks[:, :, None, :]).astype(
        jnp.bfloat16
    )
    intra_out = jnp.einsum(
        "chqk,ckhp->cqhp", mixing, x_blocks, preferred_element_type=jnp.float32
    )
    block_end = cumulative[:, :, -1]
    tail_weight = jnp.exp(block_end[:, :, None] - cumulative) * dt_blocks
    scaled_x = (x_blocks * tail_weight.transpose(0, 2, 1)[:, :, :, None]).astype(jnp.bfloat16)
    contrib = jnp.einsum(
        "ckhp,ckn->chpn", scaled_x, b_blocks, preferred_element_type=jnp.float32
    )
    decay_sum = jnp.zeros((head_count,), jnp.float32)
    running = jnp.zeros((head_count, head_size, state_size), jnp.float32)
    decay_sums = []
    runnings = []
    for c in range(block_count):
        decay_sums.append(decay_sum)
        runnings.append(running)
        running = jnp.exp(block_end[c])[:, None, None] * running + contrib[c]
        decay_sum = decay_sum + block_end[c]
    records = (intra_out, cumulative, jnp.stack(decay_sums), jnp.stack(runnings), c_blocks)
    return ((decay_sum, running), records)


def apply_state(records, incoming):
    intra_out, cumulative, decay_sums, runnings, c_blocks = records
    block_count = intra_out.shape[0]
    held_state = (
        jnp.exp(decay_sums)[:, :, None, None] * incoming[None] + runnings
    ).astype(jnp.bfloat16)
    state_out = jnp.einsum(
        "cqn,chpn->cqhp", c_blocks, held_state, preferred_element_type=jnp.float32
    )
    outputs = intra_out + state_out * jnp.exp(cumulative).transpose(0, 2, 1)[:, :, :, None]
    return outputs.reshape(block_count * BLOCK, outputs.shape[2] * outputs.shape[3])


def pool_combine(lo, hi):
    top = jnp.maximum(lo[0], hi[0])
    lo_scale = jnp.exp(lo[0] - top)
    hi_scale = jnp.exp(hi[0] - top)
    total = lo[1] * lo_scale + hi[1] * hi_scale
    summed = lo[2] * lo_scale[:, None] + hi[2] * hi_scale[:, None]
    return (top, total, summed)


def butterfly_pool(local, axis):
    count = lax.axis_size(axis)
    assert count & (count - 1) == 0
    place = lax.axis_index(axis)
    state = local
    bit = 1
    while bit < count:
        sent = (state[0], state[1], state[2].astype(jnp.bfloat16))
        perm = [(q, q ^ bit) for q in range(count)]
        received = lax.ppermute(sent, axis, perm)
        own = (sent[0], sent[1], sent[2].astype(jnp.float32))
        other = (received[0], received[1], received[2].astype(jnp.float32))
        is_low = (place & bit) == 0
        lo = jax.tree.map(lambda a, b: jnp.where(is_low, a, b), own, other)
        hi = jax.tree.map(lambda a, b: jnp.where(is_low, b, a), own, other)
        state = pool_combine(lo, hi)
        bit *= 2
    return state


def body(
    ssm_input,
    gate_input,
    state_proj,
    step_raw,
    decay_log,
    skip_gain,
    norm_gain,
    out_weight,
    latents,
    lengths,
):
    row_count = ssm_input.shape[1]
    inner_width = ssm_input.shape[2]
    head_count = decay_log.shape[1]
    head_size = inner_width // head_count
    state_size = state_proj.shape[2] // 4
    model_width = out_weight.shape[1]
    positions = lax.axis_index("seq") * row_count + jnp.arange(row_count, dtype=jnp.int32)
    is_valid = positions < lengths[0]
    step_size = jnp.where(is_valid[None, :], jax.nn.softplus(step_raw[0]), 0.0)
    decay_rates = jnp.exp(decay_log)
    flat_tokens = ssm_input[0]
    tokens = flat_tokens.reshape(row_count, head_count, head_size)
    projections = state_proj[0]
    forward_totals, forward_records = block_pass(
        tokens,
        step_size[:head_count],
        projections[:, :state_size],
        projections[:, state_size : 2 * state_size],
        decay_rates[0],
    )
    backward_totals, backward_records = block_pass(
        tokens[::-1],
        step_size[head_count:, ::-1],
        projections[::-1, 2 * state_size : 3 * state_size],
        projections[::-1, 3 * state_size :],
        decay_rates[1],
    )
    unused_item, forward_in = exclusive_scan(forward_totals, "seq", False)
    unused_item, backward_in = exclusive_scan(backward_totals, "seq", True)
    forward_out = apply_state(forward_records, forward_in)
    backward_out = apply_state(backward_records, backward_in)[::-1]
    skip_wide = jnp.repeat(skip_gain, head_size)
    mixed_out = forward_out + backward_out + skip_wide[None, :] * flat_tokens.astype(jnp.float32)
    gated_out = mixed_out * jax.nn.silu(gate_input[0].astype(jnp.float32))
    squared = (gated_out * gated_out).reshape(row_count, head_count, head_size)
    mean_square = jnp.mean(squared, axis=2)
    inverse_scale = jnp.repeat(lax.rsqrt(mean_square + 1e-05), head_size, axis=1)
    normed = (gated_out * inverse_scale * norm_gain[None, :]).astype(jnp.bfloat16)
    projected = jnp.dot(
        normed,
        lax.all_gather(out_weight, "dp", axis=0, tiled=True),
        preferred_element_type=jnp.float32,
    )
    encoded = projected.astype(jnp.bfloat16)
    score_scale = 1.0 / math.sqrt(model_width)
    scores = (
        jnp.einsum("rd,sd->rs", latents, encoded, preferred_element_type=jnp.float32) * score_scale
    )
    local_top = jnp.max(jnp.where(is_valid[None, :], scores, -1e30), axis=1)
    prob_values = jnp.where(is_valid[None, :], jnp.exp(scores - local_top[:, None]), 0.0)
    weight_sum = jnp.sum(prob_values, axis=1)
    weighted_sum = jnp.dot(
        prob_values.astype(jnp.bfloat16), encoded, preferred_element_type=jnp.float32
    )
    unused_item, total_weight, total_sum = butterfly_pool(
        (local_top, weight_sum, weighted_sum), "seq"
    )
    pooled = (total_sum / total_weight[:, None]).astype(jnp.bfloat16)
    return (encoded[None], pooled[None])


def solution(mesh):
    in_specs = (
        P("dp", "seq", None),
        P("dp", "seq", None),
        P("dp", "seq", None),
        P("dp", None, "seq"),
        P(),
        P(),
        P(),
        P("dp", None),
        P(),
        P("dp"),
    )
    out_specs = (P("dp", "seq", None), P("dp", None, None))
    return jax.shard_map(body, mesh=mesh, in_specs=in_specs, out_specs=out_specs, check_vma=False)
```

```python
import math

import jax
import jax.numpy as jnp
from jax import lax
from jax.sharding import PartitionSpec as P

BLOCK = 128


def chain_combine(earlier, later):
    return (
        earlier[0] + later[0],
        jnp.exp(later[0])[:, None, None] * earlier[1] + later[1],
    )


def exclusive_scan(part, axis, reverse):
    count = lax.axis_size(axis)
    inclusive = part
    exclusive = jax.tree.map(jnp.zeros_like, part)
    rounds = max(1, (count - 1).bit_length())
    for k in range(rounds):
        shift = 1 << k
        if shift >= count:
            break
        if reverse:
            perm = [(q, q - shift) for q in range(shift, count)]
        else:
            perm = [(q, q + shift) for q in range(count - shift)]
        sent = (inclusive[0], inclusive[1].astype(jnp.bfloat16))
        received = lax.ppermute(sent, axis, perm)
        received = (received[0], received[1].astype(jnp.float32))
        exclusive = chain_combine(received, exclusive)
        if k + 1 < rounds:
            inclusive = chain_combine(received, inclusive)
    return exclusive


def block_pass(x_seq, dt_seq, b_seq, c_seq, forget_rate):
    row_count, head_count, head_size = x_seq.shape
    state_size = b_seq.shape[1]
    block_count = row_count // BLOCK
    x_blocks = x_seq.reshape(block_count, BLOCK, head_count, head_size)
    dt_blocks = dt_seq.reshape(head_count, block_count, BLOCK).transpose(1, 0, 2)
    b_blocks = b_seq.reshape(block_count, BLOCK, state_size)
    c_blocks = c_seq.reshape(block_count, BLOCK, state_size)
    cumulative = jnp.cumsum(-dt_blocks * forget_rate[None, :, None], axis=2)
    gram_matrix = jnp.einsum(
        "cqn,ckn->cqk", c_blocks, b_blocks, preferred_element_type=jnp.float32
    )
    symbol_offset = jnp.arange(BLOCK, dtype=jnp.int32)
    causal = symbol_offset[:, None] >= symbol_offset[None, :]
    spread = jnp.where(
        causal[None, None], cumulative[:, :, :, None] - cumulative[:, :, None, :], -jnp.inf
    )
    mixing = (gram_matrix[:, None] * jnp.exp(spread) * dt_blocks[:, :, None, :]).astype(
        jnp.bfloat16
    )
    intra_out = jnp.einsum(
        "chqk,ckhp->cqhp", mixing, x_blocks, preferred_element_type=jnp.float32
    )
    block_end = cumulative[:, :, -1]
    tail_weight = jnp.exp(block_end[:, :, None] - cumulative) * dt_blocks
    scaled_x = (x_blocks * tail_weight.transpose(0, 2, 1)[:, :, :, None]).astype(jnp.bfloat16)
    contrib = jnp.einsum(
        "ckhp,ckn->chpn", scaled_x, b_blocks, preferred_element_type=jnp.float32
    )
    decay_sum = jnp.zeros((head_count,), jnp.float32)
    running = jnp.zeros((head_count, head_size, state_size), jnp.float32)
    decay_sums = []
    runnings = []
    for c in range(block_count):
        decay_sums.append(decay_sum)
        runnings.append(running)
        running = jnp.exp(block_end[c])[:, None, None] * running + contrib[c]
        decay_sum = decay_sum + block_end[c]
    records = (intra_out, cumulative, jnp.stack(decay_sums), jnp.stack(runnings), c_blocks)
    return ((decay_sum, running), records)


def apply_state(records, incoming):
    intra_out, cumulative, decay_sums, runnings, c_blocks = records
    block_count = intra_out.shape[0]
    held_state = (
        jnp.exp(decay_sums)[:, :, None, None] * incoming[None] + runnings
    ).astype(jnp.bfloat16)
    state_out = jnp.einsum(
        "cqn,chpn->cqhp", c_blocks, held_state, preferred_element_type=jnp.float32
    )
    outputs = intra_out + state_out * jnp.exp(cumulative).transpose(0, 2, 1)[:, :, :, None]
    return outputs.reshape(block_count * BLOCK, outputs.shape[2] * outputs.shape[3])


def pool_combine(lo, hi):
    top = jnp.maximum(lo[0], hi[0])
    lo_scale = jnp.exp(lo[0] - top)
    hi_scale = jnp.exp(hi[0] - top)
    total = lo[1] * lo_scale + hi[1] * hi_scale
    summed = lo[2] * lo_scale[:, None] + hi[2] * hi_scale[:, None]
    return (top, total, summed)


def xor_exchange(value, axis, bit):
    count = lax.axis_size(axis)
    return lax.ppermute(value, axis, [(q, q ^ bit) for q in range(count)])


def reduce_pool(local, axis, scatter_rounds):
    count = lax.axis_size(axis)
    assert count & (count - 1) == 0
    place = lax.axis_index(axis)
    state = local
    bit = 1
    for unused_round in range(scatter_rounds):
        if bit >= count:
            break
        half = state[0].shape[0] // 2
        upper = (place & bit) != 0
        keep = jax.tree.map(lambda a: jnp.where(upper, a[half:], a[:half]), state)
        send = jax.tree.map(lambda a: jnp.where(upper, a[:half], a[half:]), state)
        received = xor_exchange((send[0], send[1], send[2].astype(jnp.bfloat16)), axis, bit)
        other = (received[0], received[1], received[2].astype(jnp.float32))
        state = pool_combine(keep, other)
        bit *= 2
    gather_bits = []
    while bit < count:
        sent = (state[0], state[1], state[2].astype(jnp.bfloat16))
        received = xor_exchange(sent, axis, bit)
        own = (sent[0], sent[1], sent[2].astype(jnp.float32))
        other = (received[0], received[1], received[2].astype(jnp.float32))
        is_low = (place & bit) == 0
        lo = jax.tree.map(lambda a, b: jnp.where(is_low, a, b), own, other)
        hi = jax.tree.map(lambda a, b: jnp.where(is_low, b, a), own, other)
        state = pool_combine(lo, hi)
        bit *= 2
    rows = (state[2] / state[1][:, None]).astype(jnp.bfloat16)
    bit = 1
    while bit * 2 <= count and len(gather_bits) < scatter_rounds:
        gather_bits.append(bit)
        bit *= 2
    for bit in reversed(gather_bits):
        received = xor_exchange(rows, axis, bit)
        upper = (place & bit) != 0
        rows = jnp.where(
            upper,
            jnp.concatenate([received, rows], axis=0),
            jnp.concatenate([rows, received], axis=0),
        )
    return rows


def body(
    ssm_input,
    gate_input,
    state_proj,
    step_raw,
    decay_log,
    skip_gain,
    norm_gain,
    out_weight,
    latents,
    lengths,
):
    row_count = ssm_input.shape[1]
    inner_width = ssm_input.shape[2]
    head_count = decay_log.shape[1]
    head_size = inner_width // head_count
    state_size = state_proj.shape[2] // 4
    model_width = out_weight.shape[1]
    positions = lax.axis_index("seq") * row_count + jnp.arange(row_count, dtype=jnp.int32)
    is_valid = positions < lengths[0]
    step_size = jnp.where(is_valid[None, :], jax.nn.softplus(step_raw[0]), 0.0)
    decay_rates = jnp.exp(decay_log)
    flat_tokens = ssm_input[0]
    tokens = flat_tokens.reshape(row_count, head_count, head_size)
    projections = state_proj[0]
    forward_totals, forward_records = block_pass(
        tokens,
        step_size[:head_count],
        projections[:, :state_size],
        projections[:, state_size : 2 * state_size],
        decay_rates[0],
    )
    backward_totals, backward_records = block_pass(
        tokens[::-1],
        step_size[head_count:, ::-1],
        projections[::-1, 2 * state_size : 3 * state_size],
        projections[::-1, 3 * state_size :],
        decay_rates[1],
    )
    unused_item, forward_in = exclusive_scan(forward_totals, "seq", False)
    unused_item, backward_in = exclusive_scan(backward_totals, "seq", True)
    forward_out = apply_state(forward_records, forward_in)
    backward_out = apply_state(backward_records, backward_in)[::-1]
    skip_wide = jnp.repeat(skip_gain, head_size)
    mixed_out = forward_out + backward_out + skip_wide[None, :] * flat_tokens.astype(jnp.float32)
    gated_out = mixed_out * jax.nn.silu(gate_input[0].astype(jnp.float32))
    squared = (gated_out * gated_out).reshape(row_count, head_count, head_size)
    mean_square = jnp.mean(squared, axis=2)
    inverse_scale = jnp.repeat(lax.rsqrt(mean_square + 1e-05), head_size, axis=1)
    normed = (gated_out * inverse_scale * norm_gain[None, :]).astype(jnp.bfloat16)
    projected = jnp.dot(
        normed,
        lax.all_gather(out_weight, "dp", axis=0, tiled=True),
        preferred_element_type=jnp.float32,
    )
    encoded = projected.astype(jnp.bfloat16)
    score_scale = 1.0 / math.sqrt(model_width)
    scores = (
        jnp.einsum("rd,sd->rs", latents, encoded, preferred_element_type=jnp.float32) * score_scale
    )
    local_top = jnp.max(jnp.where(is_valid[None, :], scores, -1e30), axis=1)
    prob_values = jnp.where(is_valid[None, :], jnp.exp(scores - local_top[:, None]), 0.0)
    weight_sum = jnp.sum(prob_values, axis=1)
    weighted_sum = jnp.dot(
        prob_values.astype(jnp.bfloat16), encoded, preferred_element_type=jnp.float32
    )
    pooled = reduce_pool((local_top, weight_sum, weighted_sum), "seq", 3)
    return (encoded[None], pooled[None])


def solution(mesh):
    in_specs = (
        P("dp", "seq", None),
        P("dp", "seq", None),
        P("dp", "seq", None),
        P("dp", None, "seq"),
        P(),
        P(),
        P(),
        P("dp", None),
        P(),
        P("dp"),
    )
    out_specs = (P("dp", "seq", None), P("dp", None, None))
    return jax.shard_map(body, mesh=mesh, in_specs=in_specs, out_specs=out_specs, check_vma=False)
```

```python
import math

import jax
import jax.numpy as jnp
from jax import lax
from jax.sharding import PartitionSpec as P

BLOCK = 128


def chain_combine(earlier, later):
    return (
        earlier[0] + later[0],
        jnp.exp(later[0])[:, None, None] * earlier[1] + later[1],
    )


def exclusive_scans(parts, axis):
    count = lax.axis_size(axis)
    inclusive = [part for part, unused_item in parts]
    exclusive = [jax.tree.map(jnp.zeros_like, part) for part, unused_item in parts]
    rounds = max(1, (count - 1).bit_length())
    for k in range(rounds):
        shift = 1 << k
        if shift >= count:
            break
        received = []
        for i, (unused_item, reverse) in enumerate(parts):
            if reverse:
                perm = [(q, q - shift) for q in range(shift, count)]
            else:
                perm = [(q, q + shift) for q in range(count - shift)]
            sent = (inclusive[i][0], inclusive[i][1].astype(jnp.bfloat16))
            received.append(lax.ppermute(sent, axis, perm))
        received = lax.optimization_barrier(received)
        for i in range(len(parts)):
            got = (received[i][0], received[i][1].astype(jnp.float32))
            exclusive[i] = chain_combine(got, exclusive[i])
            if k + 1 < rounds:
                inclusive[i] = chain_combine(got, inclusive[i])
    return exclusive


def block_pass(x_seq, dt_seq, b_seq, c_seq, forget_rate):
    row_count, head_count, head_size = x_seq.shape
    state_size = b_seq.shape[1]
    block_count = row_count // BLOCK
    x_blocks = x_seq.reshape(block_count, BLOCK, head_count, head_size)
    dt_blocks = dt_seq.reshape(head_count, block_count, BLOCK).transpose(1, 0, 2)
    b_blocks = b_seq.reshape(block_count, BLOCK, state_size)
    c_blocks = c_seq.reshape(block_count, BLOCK, state_size)
    cumulative = jnp.cumsum(-dt_blocks * forget_rate[None, :, None], axis=2)
    gram_matrix = jnp.einsum(
        "cqn,ckn->cqk", c_blocks, b_blocks, preferred_element_type=jnp.float32
    )
    symbol_offset = jnp.arange(BLOCK, dtype=jnp.int32)
    causal = symbol_offset[:, None] >= symbol_offset[None, :]
    spread = jnp.where(
        causal[None, None], cumulative[:, :, :, None] - cumulative[:, :, None, :], -jnp.inf
    )
    mixing = (gram_matrix[:, None] * jnp.exp(spread) * dt_blocks[:, :, None, :]).astype(
        jnp.bfloat16
    )
    intra_out = jnp.einsum(
        "chqk,ckhp->cqhp", mixing, x_blocks, preferred_element_type=jnp.float32
    )
    block_end = cumulative[:, :, -1]
    tail_weight = jnp.exp(block_end[:, :, None] - cumulative) * dt_blocks
    scaled_x = (x_blocks * tail_weight.transpose(0, 2, 1)[:, :, :, None]).astype(jnp.bfloat16)
    contrib = jnp.einsum(
        "ckhp,ckn->chpn", scaled_x, b_blocks, preferred_element_type=jnp.float32
    )
    decay_sum = jnp.zeros((head_count,), jnp.float32)
    running = jnp.zeros((head_count, head_size, state_size), jnp.float32)
    decay_sums = []
    runnings = []
    for c in range(block_count):
        decay_sums.append(decay_sum)
        runnings.append(running)
        running = jnp.exp(block_end[c])[:, None, None] * running + contrib[c]
        decay_sum = decay_sum + block_end[c]
    records = (intra_out, cumulative, jnp.stack(decay_sums), jnp.stack(runnings), c_blocks)
    return ((decay_sum, running), records)


def apply_state(records, incoming):
    intra_out, cumulative, decay_sums, runnings, c_blocks = records
    block_count = intra_out.shape[0]
    held_state = (
        jnp.exp(decay_sums)[:, :, None, None] * incoming[None] + runnings
    ).astype(jnp.bfloat16)
    state_out = jnp.einsum(
        "cqn,chpn->cqhp", c_blocks, held_state, preferred_element_type=jnp.float32
    )
    outputs = intra_out + state_out * jnp.exp(cumulative).transpose(0, 2, 1)[:, :, :, None]
    return outputs.reshape(block_count * BLOCK, outputs.shape[2] * outputs.shape[3])


def pool_combine(lo, hi):
    top = jnp.maximum(lo[0], hi[0])
    lo_scale = jnp.exp(lo[0] - top)
    hi_scale = jnp.exp(hi[0] - top)
    total = lo[1] * lo_scale + hi[1] * hi_scale
    summed = lo[2] * lo_scale[:, None] + hi[2] * hi_scale[:, None]
    return (top, total, summed)


def xor_exchange(value, axis, bit):
    count = lax.axis_size(axis)
    return lax.ppermute(value, axis, [(q, q ^ bit) for q in range(count)])


def reduce_pool(local, axis, scatter_rounds):
    count = lax.axis_size(axis)
    assert count & (count - 1) == 0
    place = lax.axis_index(axis)
    state = local
    bit = 1
    for unused_round in range(scatter_rounds):
        if bit >= count:
            break
        half = state[0].shape[0] // 2
        upper = (place & bit) != 0
        keep = jax.tree.map(lambda a: jnp.where(upper, a[half:], a[:half]), state)
        send = jax.tree.map(lambda a: jnp.where(upper, a[:half], a[half:]), state)
        received = xor_exchange((send[0], send[1], send[2].astype(jnp.bfloat16)), axis, bit)
        other = (received[0], received[1], received[2].astype(jnp.float32))
        state = pool_combine(keep, other)
        bit *= 2
    gather_bits = []
    while bit < count:
        sent = (state[0], state[1], state[2].astype(jnp.bfloat16))
        received = xor_exchange(sent, axis, bit)
        own = (sent[0], sent[1], sent[2].astype(jnp.float32))
        other = (received[0], received[1], received[2].astype(jnp.float32))
        is_low = (place & bit) == 0
        lo = jax.tree.map(lambda a, b: jnp.where(is_low, a, b), own, other)
        hi = jax.tree.map(lambda a, b: jnp.where(is_low, b, a), own, other)
        state = pool_combine(lo, hi)
        bit *= 2
    rows = (state[2] / state[1][:, None]).astype(jnp.bfloat16)
    bit = 1
    while bit * 2 <= count and len(gather_bits) < scatter_rounds:
        gather_bits.append(bit)
        bit *= 2
    for bit in reversed(gather_bits):
        received = xor_exchange(rows, axis, bit)
        upper = (place & bit) != 0
        rows = jnp.where(
            upper,
            jnp.concatenate([received, rows], axis=0),
            jnp.concatenate([rows, received], axis=0),
        )
    return rows


def all_to_all_pool(local, axis):
    count = lax.axis_size(axis)
    local_top, weight_sum, weighted_sum = local
    row_total, width = weighted_sum.shape
    rows = row_total // count
    moved = lax.all_to_all(
        weighted_sum.astype(jnp.bfloat16), axis, 0, 0, tiled=True
    ).reshape(count, rows, width)
    stats = lax.all_to_all(
        jnp.stack([local_top, weight_sum], axis=0), axis, 1, 1, tiled=True
    ).reshape(2, count, rows)
    top = jnp.max(stats[0], axis=0)
    scale = jnp.exp(stats[0] - top[None, :])
    total = jnp.sum(stats[1] * scale, axis=0)
    summed = jnp.sum(moved.astype(jnp.float32) * scale[:, :, None], axis=0)
    finished = (summed / total[:, None]).astype(jnp.bfloat16)
    return lax.all_gather(finished, axis, axis=0, tiled=True)


def body(
    ssm_input,
    gate_input,
    state_proj,
    step_raw,
    decay_log,
    skip_gain,
    norm_gain,
    out_weight,
    latents,
    lengths,
):
    row_count = ssm_input.shape[1]
    inner_width = ssm_input.shape[2]
    head_count = decay_log.shape[1]
    head_size = inner_width // head_count
    state_size = state_proj.shape[2] // 4
    model_width = out_weight.shape[1]
    positions = lax.axis_index("seq") * row_count + jnp.arange(row_count, dtype=jnp.int32)
    is_valid = positions < lengths[0]
    step_size = jnp.where(is_valid[None, :], jax.nn.softplus(step_raw[0]), 0.0)
    decay_rates = jnp.exp(decay_log)
    flat_tokens = ssm_input[0]
    tokens = flat_tokens.reshape(row_count, head_count, head_size)
    projections = state_proj[0]
    forward_totals, forward_records = block_pass(
        tokens,
        step_size[:head_count],
        projections[:, :state_size],
        projections[:, state_size : 2 * state_size],
        decay_rates[0],
    )
    backward_totals, backward_records = block_pass(
        tokens[::-1],
        step_size[head_count:, ::-1],
        projections[::-1, 2 * state_size : 3 * state_size],
        projections[::-1, 3 * state_size :],
        decay_rates[1],
    )
    (unused_item, forward_in), (unused_item, backward_in) = exclusive_scans(
        [(forward_totals, False), (backward_totals, True)], "seq"
    )
    forward_out = apply_state(forward_records, forward_in)
    backward_out = apply_state(backward_records, backward_in)[::-1]
    skip_wide = jnp.repeat(skip_gain, head_size)
    mixed_out = forward_out + backward_out + skip_wide[None, :] * flat_tokens.astype(jnp.float32)
    gated_out = mixed_out * jax.nn.silu(gate_input[0].astype(jnp.float32))
    squared = (gated_out * gated_out).reshape(row_count, head_count, head_size)
    mean_square = jnp.mean(squared, axis=2)
    inverse_scale = jnp.repeat(lax.rsqrt(mean_square + 1e-05), head_size, axis=1)
    normed = (gated_out * inverse_scale * norm_gain[None, :]).astype(jnp.bfloat16)
    projected = jnp.dot(
        normed,
        lax.all_gather(out_weight, "dp", axis=0, tiled=True),
        preferred_element_type=jnp.float32,
    )
    encoded = projected.astype(jnp.bfloat16)
    score_scale = 1.0 / math.sqrt(model_width)
    scores = (
        jnp.einsum("rd,sd->rs", latents, encoded, preferred_element_type=jnp.float32) * score_scale
    )
    local_top = jnp.max(jnp.where(is_valid[None, :], scores, -1e30), axis=1)
    prob_values = jnp.where(is_valid[None, :], jnp.exp(scores - local_top[:, None]), 0.0)
    weight_sum = jnp.sum(prob_values, axis=1)
    weighted_sum = jnp.dot(
        prob_values.astype(jnp.bfloat16), encoded, preferred_element_type=jnp.float32
    )
    pooled = all_to_all_pool((local_top, weight_sum, weighted_sum), "seq")
    return (encoded[None], pooled[None])


def solution(mesh):
    in_specs = (
        P("dp", "seq", None),
        P("dp", "seq", None),
        P("dp", "seq", None),
        P("dp", None, "seq"),
        P(),
        P(),
        P(),
        P("dp", None),
        P(),
        P("dp"),
    )
    out_specs = (P("dp", "seq", None), P("dp", None, None))
    return jax.shard_map(body, mesh=mesh, in_specs=in_specs, out_specs=out_specs, check_vma=False)
```

```python
import math

import jax
import jax.numpy as jnp
from jax import lax
from jax.sharding import PartitionSpec as P

BLOCK = 128


def chain_combine(earlier, later):
    return (
        earlier[0] + later[0],
        jnp.exp(later[0])[:, None, None] * earlier[1] + later[1],
    )


def exclusive_scans(parts, axis):
    count = lax.axis_size(axis)
    inclusive = [part for part, unused_item in parts]
    exclusive = [jax.tree.map(jnp.zeros_like, part) for part, unused_item in parts]
    rounds = max(1, (count - 1).bit_length())
    for k in range(rounds):
        shift = 1 << k
        if shift >= count:
            break
        received = []
        for i, (unused_item, reverse) in enumerate(parts):
            if reverse:
                perm = [(q, q - shift) for q in range(shift, count)]
            else:
                perm = [(q, q + shift) for q in range(count - shift)]
            sent = (inclusive[i][0], inclusive[i][1].astype(jnp.bfloat16))
            received.append(lax.ppermute(sent, axis, perm))
        received = lax.optimization_barrier(received)
        for i in range(len(parts)):
            got = (received[i][0], received[i][1].astype(jnp.float32))
            exclusive[i] = chain_combine(got, exclusive[i])
            if k + 1 < rounds:
                inclusive[i] = chain_combine(got, inclusive[i])
    return exclusive


def block_pass(x_seq, dt_seq, b_seq, c_seq, forget_rate):
    row_count, head_count, head_size = x_seq.shape
    state_size = b_seq.shape[1]
    block_count = row_count // BLOCK
    x_blocks = x_seq.reshape(block_count, BLOCK, head_count, head_size)
    dt_blocks = dt_seq.reshape(head_count, block_count, BLOCK).transpose(1, 0, 2)
    b_blocks = b_seq.reshape(block_count, BLOCK, state_size)
    c_blocks = c_seq.reshape(block_count, BLOCK, state_size)
    cumulative = jnp.cumsum(-dt_blocks * forget_rate[None, :, None], axis=2)
    gram_matrix = jnp.einsum(
        "cqn,ckn->cqk", c_blocks, b_blocks, preferred_element_type=jnp.float32
    )
    symbol_offset = jnp.arange(BLOCK, dtype=jnp.int32)
    causal = symbol_offset[:, None] >= symbol_offset[None, :]
    spread = jnp.where(
        causal[None, None], cumulative[:, :, :, None] - cumulative[:, :, None, :], -jnp.inf
    )
    mixing = (gram_matrix[:, None] * jnp.exp(spread) * dt_blocks[:, :, None, :]).astype(
        jnp.bfloat16
    )
    intra_out = jnp.einsum(
        "chqk,ckhp->cqhp", mixing, x_blocks, preferred_element_type=jnp.float32
    )
    block_end = cumulative[:, :, -1]
    tail_weight = jnp.exp(block_end[:, :, None] - cumulative) * dt_blocks
    scaled_x = (x_blocks * tail_weight.transpose(0, 2, 1)[:, :, :, None]).astype(jnp.bfloat16)
    contrib = jnp.einsum(
        "ckhp,ckn->chpn", scaled_x, b_blocks, preferred_element_type=jnp.float32
    )
    decay_sum = jnp.zeros((head_count,), jnp.float32)
    running = jnp.zeros((head_count, head_size, state_size), jnp.float32)
    decay_sums = []
    runnings = []
    for c in range(block_count):
        decay_sums.append(decay_sum)
        runnings.append(running)
        running = jnp.exp(block_end[c])[:, None, None] * running + contrib[c]
        decay_sum = decay_sum + block_end[c]
    records = (intra_out, cumulative, jnp.stack(decay_sums), jnp.stack(runnings), c_blocks)
    return ((decay_sum, running), records)


def apply_state(records, incoming):
    intra_out, cumulative, decay_sums, runnings, c_blocks = records
    block_count = intra_out.shape[0]
    held_state = (
        jnp.exp(decay_sums)[:, :, None, None] * incoming[None] + runnings
    ).astype(jnp.bfloat16)
    state_out = jnp.einsum(
        "cqn,chpn->cqhp", c_blocks, held_state, preferred_element_type=jnp.float32
    )
    outputs = intra_out + state_out * jnp.exp(cumulative).transpose(0, 2, 1)[:, :, :, None]
    return outputs.reshape(block_count * BLOCK, outputs.shape[2] * outputs.shape[3])


def pool_combine(lo, hi):
    top = jnp.maximum(lo[0], hi[0])
    lo_scale = jnp.exp(lo[0] - top)
    hi_scale = jnp.exp(hi[0] - top)
    total = lo[1] * lo_scale + hi[1] * hi_scale
    summed = lo[2] * lo_scale[:, None] + hi[2] * hi_scale[:, None]
    return (top, total, summed)


def xor_exchange(value, axis, bit):
    count = lax.axis_size(axis)
    return lax.ppermute(value, axis, [(q, q ^ bit) for q in range(count)])


def reduce_pool(local, axis, scatter_rounds):
    count = lax.axis_size(axis)
    assert count & (count - 1) == 0
    place = lax.axis_index(axis)
    state = local
    bit = 1
    for unused_round in range(scatter_rounds):
        if bit >= count:
            break
        half = state[0].shape[0] // 2
        upper = (place & bit) != 0
        keep = jax.tree.map(lambda a: jnp.where(upper, a[half:], a[:half]), state)
        send = jax.tree.map(lambda a: jnp.where(upper, a[:half], a[half:]), state)
        received = xor_exchange((send[0], send[1], send[2].astype(jnp.bfloat16)), axis, bit)
        other = (received[0], received[1], received[2].astype(jnp.float32))
        state = pool_combine(keep, other)
        bit *= 2
    gather_bits = []
    while bit < count:
        sent = (state[0], state[1], state[2].astype(jnp.bfloat16))
        received = xor_exchange(sent, axis, bit)
        own = (sent[0], sent[1], sent[2].astype(jnp.float32))
        other = (received[0], received[1], received[2].astype(jnp.float32))
        is_low = (place & bit) == 0
        lo = jax.tree.map(lambda a, b: jnp.where(is_low, a, b), own, other)
        hi = jax.tree.map(lambda a, b: jnp.where(is_low, b, a), own, other)
        state = pool_combine(lo, hi)
        bit *= 2
    rows = (state[2] / state[1][:, None]).astype(jnp.bfloat16)
    bit = 1
    while bit * 2 <= count and len(gather_bits) < scatter_rounds:
        gather_bits.append(bit)
        bit *= 2
    for bit in reversed(gather_bits):
        received = xor_exchange(rows, axis, bit)
        upper = (place & bit) != 0
        rows = jnp.where(
            upper,
            jnp.concatenate([received, rows], axis=0),
            jnp.concatenate([rows, received], axis=0),
        )
    return rows


def split_wide(values):
    high = values.astype(jnp.bfloat16)
    low = (values - high.astype(jnp.float32)).astype(jnp.bfloat16)
    return high, low


def all_to_all_pool(local, axis):
    count = lax.axis_size(axis)
    local_top, weight_sum, weighted_sum = local
    row_total, width = weighted_sum.shape
    rows = row_total // count
    stats = jnp.stack(split_wide(local_top) + split_wide(weight_sum), axis=0)
    stats = stats.reshape(4, count, rows).transpose(1, 0, 2).reshape(count, 4 * rows)
    pad = (-4 * rows) % 128
    packed = jnp.concatenate(
        [
            weighted_sum.astype(jnp.bfloat16).reshape(count, rows * width),
            jnp.pad(stats, ((0, 0), (0, pad))),
        ],
        axis=1,
    )
    moved = lax.all_to_all(packed, axis, 0, 0, tiled=True)
    parts = moved[:, : rows * width].reshape(count, rows, width).astype(jnp.float32)
    got = moved[:, rows * width : rows * width + 4 * rows].astype(jnp.float32)
    got = got.reshape(count, 4, rows)
    tops = got[:, 0] + got[:, 1]
    totals = got[:, 2] + got[:, 3]
    top = jnp.max(tops, axis=0)
    scale = jnp.exp(tops - top[None, :])
    total = jnp.sum(totals * scale, axis=0)
    summed = jnp.sum(parts * scale[:, :, None], axis=0)
    finished = (summed / total[:, None]).astype(jnp.bfloat16)
    spread_rows = jnp.broadcast_to(finished[None], (count, rows, width))
    gathered = lax.all_to_all(spread_rows, axis, 0, 0, tiled=True)
    return gathered.reshape(row_total, width)


def body(
    ssm_input,
    gate_input,
    state_proj,
    step_raw,
    decay_log,
    skip_gain,
    norm_gain,
    out_weight,
    latents,
    lengths,
):
    row_count = ssm_input.shape[1]
    inner_width = ssm_input.shape[2]
    head_count = decay_log.shape[1]
    head_size = inner_width // head_count
    state_size = state_proj.shape[2] // 4
    model_width = out_weight.shape[1]
    positions = lax.axis_index("seq") * row_count + jnp.arange(row_count, dtype=jnp.int32)
    is_valid = positions < lengths[0]
    step_size = jnp.where(is_valid[None, :], jax.nn.softplus(step_raw[0]), 0.0)
    decay_rates = jnp.exp(decay_log)
    flat_tokens = ssm_input[0]
    tokens = flat_tokens.reshape(row_count, head_count, head_size)
    projections = state_proj[0]
    forward_totals, forward_records = block_pass(
        tokens,
        step_size[:head_count],
        projections[:, :state_size],
        projections[:, state_size : 2 * state_size],
        decay_rates[0],
    )
    backward_totals, backward_records = block_pass(
        tokens[::-1],
        step_size[head_count:, ::-1],
        projections[::-1, 2 * state_size : 3 * state_size],
        projections[::-1, 3 * state_size :],
        decay_rates[1],
    )
    (unused_item, forward_in), (unused_item, backward_in) = exclusive_scans(
        [(forward_totals, False), (backward_totals, True)], "seq"
    )
    forward_out = apply_state(forward_records, forward_in)
    backward_out = apply_state(backward_records, backward_in)[::-1]
    skip_wide = jnp.repeat(skip_gain, head_size)
    mixed_out = forward_out + backward_out + skip_wide[None, :] * flat_tokens.astype(jnp.float32)
    gated_out = mixed_out * jax.nn.silu(gate_input[0].astype(jnp.float32))
    squared = (gated_out * gated_out).reshape(row_count, head_count, head_size)
    mean_square = jnp.mean(squared, axis=2)
    inverse_scale = jnp.repeat(lax.rsqrt(mean_square + 1e-05), head_size, axis=1)
    normed = (gated_out * inverse_scale * norm_gain[None, :]).astype(jnp.bfloat16)
    projected = jnp.dot(
        normed,
        lax.all_gather(out_weight, "dp", axis=0, tiled=True),
        preferred_element_type=jnp.float32,
    )
    encoded = projected.astype(jnp.bfloat16)
    score_scale = 1.0 / math.sqrt(model_width)
    scores = (
        jnp.einsum("rd,sd->rs", latents, encoded, preferred_element_type=jnp.float32) * score_scale
    )
    local_top = jnp.max(jnp.where(is_valid[None, :], scores, -1e30), axis=1)
    prob_values = jnp.where(is_valid[None, :], jnp.exp(scores - local_top[:, None]), 0.0)
    weight_sum = jnp.sum(prob_values, axis=1)
    weighted_sum = jnp.dot(
        prob_values.astype(jnp.bfloat16), encoded, preferred_element_type=jnp.float32
    )
    pooled = all_to_all_pool((local_top, weight_sum, weighted_sum), "seq")
    return (encoded[None], pooled[None])


def solution(mesh):
    in_specs = (
        P("dp", "seq", None),
        P("dp", "seq", None),
        P("dp", "seq", None),
        P("dp", None, "seq"),
        P(),
        P(),
        P(),
        P("dp", None),
        P(),
        P("dp"),
    )
    out_specs = (P("dp", "seq", None), P("dp", None, None))
    return jax.shard_map(body, mesh=mesh, in_specs=in_specs, out_specs=out_specs, check_vma=False)
```

```python
import math

import jax
import jax.numpy as jnp
from jax import lax
from jax.sharding import PartitionSpec as P

BLOCK = 128


def chain_combine(earlier, later):
    return (
        earlier[0] + later[0],
        jnp.exp(later[0])[:, None, None] * earlier[1] + later[1],
    )


def exclusive_scans(parts, axis):
    count = lax.axis_size(axis)
    inclusive = [part for part, unused_item in parts]
    exclusive = [jax.tree.map(jnp.zeros_like, part) for part, unused_item in parts]
    rounds = max(1, (count - 1).bit_length())
    for k in range(rounds):
        shift = 1 << k
        if shift >= count:
            break
        received = []
        for i, (unused_item, reverse) in enumerate(parts):
            if reverse:
                perm = [(q, q - shift) for q in range(shift, count)]
            else:
                perm = [(q, q + shift) for q in range(count - shift)]
            sent = (inclusive[i][0], inclusive[i][1].astype(jnp.bfloat16))
            received.append(lax.ppermute(sent, axis, perm))
        received = lax.optimization_barrier(received)
        for i in range(len(parts)):
            got = (received[i][0], received[i][1].astype(jnp.float32))
            exclusive[i] = chain_combine(got, exclusive[i])
            if k + 1 < rounds:
                inclusive[i] = chain_combine(got, inclusive[i])
    return exclusive


def block_pass(x_seq, dt_seq, b_seq, c_seq, forget_rate):
    row_count, head_count, head_size = x_seq.shape
    state_size = b_seq.shape[1]
    block_count = row_count // BLOCK
    x_blocks = x_seq.reshape(block_count, BLOCK, head_count, head_size)
    dt_blocks = dt_seq.reshape(head_count, block_count, BLOCK).transpose(1, 0, 2)
    b_blocks = b_seq.reshape(block_count, BLOCK, state_size)
    c_blocks = c_seq.reshape(block_count, BLOCK, state_size)
    cumulative = jnp.cumsum(-dt_blocks * forget_rate[None, :, None], axis=2)
    gram_matrix = jnp.einsum(
        "cqn,ckn->cqk", c_blocks, b_blocks, preferred_element_type=jnp.float32
    )
    symbol_offset = jnp.arange(BLOCK, dtype=jnp.int32)
    causal = symbol_offset[:, None] >= symbol_offset[None, :]
    spread = jnp.where(
        causal[None, None], cumulative[:, :, :, None] - cumulative[:, :, None, :], -jnp.inf
    )
    mixing = (gram_matrix[:, None] * jnp.exp(spread) * dt_blocks[:, :, None, :]).astype(
        jnp.bfloat16
    )
    intra_out = jnp.einsum(
        "chqk,ckhp->cqhp", mixing, x_blocks, preferred_element_type=jnp.float32
    )
    block_end = cumulative[:, :, -1]
    tail_weight = jnp.exp(block_end[:, :, None] - cumulative) * dt_blocks
    scaled_x = (x_blocks * tail_weight.transpose(0, 2, 1)[:, :, :, None]).astype(jnp.bfloat16)
    contrib = jnp.einsum(
        "ckhp,ckn->chpn", scaled_x, b_blocks, preferred_element_type=jnp.float32
    )
    decay_sum = jnp.zeros((head_count,), jnp.float32)
    running = jnp.zeros((head_count, head_size, state_size), jnp.float32)
    decay_sums = []
    runnings = []
    for c in range(block_count):
        decay_sums.append(decay_sum)
        runnings.append(running)
        running = jnp.exp(block_end[c])[:, None, None] * running + contrib[c]
        decay_sum = decay_sum + block_end[c]
    records = (intra_out, cumulative, jnp.stack(decay_sums), jnp.stack(runnings), c_blocks)
    return ((decay_sum, running), records)


def apply_state(records, incoming):
    intra_out, cumulative, decay_sums, runnings, c_blocks = records
    block_count = intra_out.shape[0]
    held_state = (
        jnp.exp(decay_sums)[:, :, None, None] * incoming[None] + runnings
    ).astype(jnp.bfloat16)
    state_out = jnp.einsum(
        "cqn,chpn->cqhp", c_blocks, held_state, preferred_element_type=jnp.float32
    )
    outputs = intra_out + state_out * jnp.exp(cumulative).transpose(0, 2, 1)[:, :, :, None]
    return outputs.reshape(block_count * BLOCK, outputs.shape[2] * outputs.shape[3])


def pool_combine(lo, hi):
    top = jnp.maximum(lo[0], hi[0])
    lo_scale = jnp.exp(lo[0] - top)
    hi_scale = jnp.exp(hi[0] - top)
    total = lo[1] * lo_scale + hi[1] * hi_scale
    summed = lo[2] * lo_scale[:, None] + hi[2] * hi_scale[:, None]
    return (top, total, summed)


def xor_exchange(value, axis, bit):
    count = lax.axis_size(axis)
    return lax.ppermute(value, axis, [(q, q ^ bit) for q in range(count)])


def reduce_pool(local, axis, scatter_rounds):
    count = lax.axis_size(axis)
    assert count & (count - 1) == 0
    place = lax.axis_index(axis)
    state = local
    bit = 1
    for unused_round in range(scatter_rounds):
        if bit >= count:
            break
        half = state[0].shape[0] // 2
        upper = (place & bit) != 0
        keep = jax.tree.map(lambda a: jnp.where(upper, a[half:], a[:half]), state)
        send = jax.tree.map(lambda a: jnp.where(upper, a[:half], a[half:]), state)
        received = xor_exchange((send[0], send[1], send[2].astype(jnp.bfloat16)), axis, bit)
        other = (received[0], received[1], received[2].astype(jnp.float32))
        state = pool_combine(keep, other)
        bit *= 2
    gather_bits = []
    while bit < count:
        sent = (state[0], state[1], state[2].astype(jnp.bfloat16))
        received = xor_exchange(sent, axis, bit)
        own = (sent[0], sent[1], sent[2].astype(jnp.float32))
        other = (received[0], received[1], received[2].astype(jnp.float32))
        is_low = (place & bit) == 0
        lo = jax.tree.map(lambda a, b: jnp.where(is_low, a, b), own, other)
        hi = jax.tree.map(lambda a, b: jnp.where(is_low, b, a), own, other)
        state = pool_combine(lo, hi)
        bit *= 2
    rows = (state[2] / state[1][:, None]).astype(jnp.bfloat16)
    bit = 1
    while bit * 2 <= count and len(gather_bits) < scatter_rounds:
        gather_bits.append(bit)
        bit *= 2
    for bit in reversed(gather_bits):
        received = xor_exchange(rows, axis, bit)
        upper = (place & bit) != 0
        rows = jnp.where(
            upper,
            jnp.concatenate([received, rows], axis=0),
            jnp.concatenate([rows, received], axis=0),
        )
    return rows


def split_wide(values):
    rounded = lax.reduce_precision(values, exponent_bits=8, mantissa_bits=7)
    low = (values - rounded).astype(jnp.bfloat16)
    return rounded.astype(jnp.bfloat16), low


def all_to_all_pool(local, axis):
    count = lax.axis_size(axis)
    local_top, weight_sum, weighted_sum = local
    row_total, width = weighted_sum.shape
    rows = row_total // count
    stats = jnp.stack(split_wide(local_top) + split_wide(weight_sum), axis=0)
    stats = stats.reshape(4, count, rows).transpose(1, 0, 2).reshape(count, 4 * rows)
    pad = (-4 * rows) % 128
    packed = jnp.concatenate(
        [
            weighted_sum.astype(jnp.bfloat16).reshape(count, rows * width),
            jnp.pad(stats, ((0, 0), (0, pad))),
        ],
        axis=1,
    )
    moved = lax.all_to_all(packed, axis, 0, 0, tiled=True)
    parts = moved[:, : rows * width].reshape(count, rows, width).astype(jnp.float32)
    got = moved[:, rows * width : rows * width + 4 * rows].astype(jnp.float32)
    got = got.reshape(count, 4, rows)
    tops = got[:, 0] + got[:, 1]
    totals = got[:, 2] + got[:, 3]
    top = jnp.max(tops, axis=0)
    scale = jnp.exp(tops - top[None, :])
    total = jnp.sum(totals * scale, axis=0)
    summed = jnp.sum(parts * scale[:, :, None], axis=0)
    finished = (summed / total[:, None]).astype(jnp.bfloat16)
    spread_rows = jnp.broadcast_to(finished[None], (count, rows, width))
    gathered = lax.all_to_all(spread_rows, axis, 0, 0, tiled=True)
    return gathered.reshape(row_total, width)


def body(
    ssm_input,
    gate_input,
    state_proj,
    step_raw,
    decay_log,
    skip_gain,
    norm_gain,
    out_weight,
    latents,
    lengths,
):
    row_count = ssm_input.shape[1]
    inner_width = ssm_input.shape[2]
    head_count = decay_log.shape[1]
    head_size = inner_width // head_count
    state_size = state_proj.shape[2] // 4
    model_width = out_weight.shape[1]
    positions = lax.axis_index("seq") * row_count + jnp.arange(row_count, dtype=jnp.int32)
    is_valid = positions < lengths[0]
    step_size = jnp.where(is_valid[None, :], jax.nn.softplus(step_raw[0]), 0.0)
    decay_rates = jnp.exp(decay_log)
    flat_tokens = ssm_input[0]
    tokens = flat_tokens.reshape(row_count, head_count, head_size)
    projections = state_proj[0]
    forward_totals, forward_records = block_pass(
        tokens,
        step_size[:head_count],
        projections[:, :state_size],
        projections[:, state_size : 2 * state_size],
        decay_rates[0],
    )
    backward_totals, backward_records = block_pass(
        tokens[::-1],
        step_size[head_count:, ::-1],
        projections[::-1, 2 * state_size : 3 * state_size],
        projections[::-1, 3 * state_size :],
        decay_rates[1],
    )
    (unused_item, forward_in), (unused_item, backward_in) = exclusive_scans(
        [(forward_totals, False), (backward_totals, True)], "seq"
    )
    forward_out = apply_state(forward_records, forward_in)
    backward_out = apply_state(backward_records, backward_in)[::-1]
    skip_wide = jnp.repeat(skip_gain, head_size)
    mixed_out = forward_out + backward_out + skip_wide[None, :] * flat_tokens.astype(jnp.float32)
    gated_out = mixed_out * jax.nn.silu(gate_input[0].astype(jnp.float32))
    squared = (gated_out * gated_out).reshape(row_count, head_count, head_size)
    mean_square = jnp.mean(squared, axis=2)
    inverse_scale = jnp.repeat(lax.rsqrt(mean_square + 1e-05), head_size, axis=1)
    normed = (gated_out * inverse_scale * norm_gain[None, :]).astype(jnp.bfloat16)
    projected = jnp.dot(
        normed,
        lax.all_gather(out_weight, "dp", axis=0, tiled=True),
        preferred_element_type=jnp.float32,
    )
    encoded = projected.astype(jnp.bfloat16)
    score_scale = 1.0 / math.sqrt(model_width)
    scores = (
        jnp.einsum("rd,sd->rs", latents, encoded, preferred_element_type=jnp.float32) * score_scale
    )
    local_top = jnp.max(jnp.where(is_valid[None, :], scores, -1e30), axis=1)
    prob_values = jnp.where(is_valid[None, :], jnp.exp(scores - local_top[:, None]), 0.0)
    weight_sum = jnp.sum(prob_values, axis=1)
    weighted_sum = jnp.dot(
        prob_values.astype(jnp.bfloat16), encoded, preferred_element_type=jnp.float32
    )
    pooled = all_to_all_pool((local_top, weight_sum, weighted_sum), "seq")
    return (encoded[None], pooled[None])


def solution(mesh):
    in_specs = (
        P("dp", "seq", None),
        P("dp", "seq", None),
        P("dp", "seq", None),
        P("dp", None, "seq"),
        P(),
        P(),
        P(),
        P("dp", None),
        P(),
        P("dp"),
    )
    out_specs = (P("dp", "seq", None), P("dp", None, None))
    return jax.shard_map(body, mesh=mesh, in_specs=in_specs, out_specs=out_specs, check_vma=False)
```

```python
import math

import jax
import jax.numpy as jnp
from jax import lax
from jax.sharding import PartitionSpec as P

BLOCK = 128


def chain_combine(earlier, later):
    return (
        earlier[0] + later[0],
        jnp.exp(later[0])[:, None, None] * earlier[1] + later[1],
    )


def exclusive_scans(parts, axis):
    count = lax.axis_size(axis)
    inclusive = [part for part, unused_item in parts]
    exclusive = [jax.tree.map(jnp.zeros_like, part) for part, unused_item in parts]
    rounds = max(1, (count - 1).bit_length())
    for k in range(rounds):
        shift = 1 << k
        if shift >= count:
            break
        received = []
        for i, (unused_item, reverse) in enumerate(parts):
            if reverse:
                perm = [(q, q - shift) for q in range(shift, count)]
            else:
                perm = [(q, q + shift) for q in range(count - shift)]
            sent = (inclusive[i][0], inclusive[i][1].astype(jnp.bfloat16))
            received.append(lax.ppermute(sent, axis, perm))
        received = lax.optimization_barrier(received)
        for i in range(len(parts)):
            got = (received[i][0], received[i][1].astype(jnp.float32))
            exclusive[i] = chain_combine(got, exclusive[i])
            if k + 1 < rounds:
                inclusive[i] = chain_combine(got, inclusive[i])
    return exclusive


def split_wide(values):
    rounded = lax.reduce_precision(values, exponent_bits=8, mantissa_bits=7)
    low = (values - rounded).astype(jnp.bfloat16)
    return rounded.astype(jnp.bfloat16), low


def transposed_scans(forward_totals, backward_totals, axis):
    count = lax.axis_size(axis)
    head_count, head_size, state_size = forward_totals[1].shape
    assert count % head_count == 0
    per_head = count // head_count
    chunk = head_size * state_size // per_head
    head_of = jnp.arange(count, dtype=jnp.int32) // per_head

    def pack(totals):
        flat = totals[1].astype(jnp.bfloat16).reshape(count, chunk)
        high, low = split_wide(totals[0][head_of])
        tail = jnp.zeros((count, 128), jnp.bfloat16).at[:, 0].set(high).at[:, 1].set(low)
        return jnp.concatenate([flat, tail], axis=1)

    width = chunk + 128
    got = lax.all_to_all(
        jnp.concatenate([pack(forward_totals), pack(backward_totals)], axis=1),
        axis,
        0,
        0,
        tiled=True,
    )

    def unpack(block):
        decay = block[:, chunk].astype(jnp.float32) + block[:, chunk + 1].astype(jnp.float32)
        return decay, block[:, :chunk].astype(jnp.float32)

    forward_decay, forward_parts = unpack(got[:, :width])
    backward_decay, backward_parts = unpack(got[:, width:])
    place = jnp.arange(count, dtype=jnp.int32)
    dest = place[:, None, None]
    source = place[None, :, None]
    between = place[None, None, :]
    forward_span = jnp.sum(
        jnp.where((source < between) & (between < dest), forward_decay[None, None, :], 0.0),
        axis=2,
    )
    forward_weight = jnp.where(place[None, :] < place[:, None], jnp.exp(forward_span), 0.0)
    backward_span = jnp.sum(
        jnp.where((dest < between) & (between < source), backward_decay[None, None, :], 0.0),
        axis=2,
    )
    backward_weight = jnp.where(place[None, :] > place[:, None], jnp.exp(backward_span), 0.0)
    forward_in = jnp.dot(
        forward_weight, forward_parts, precision=lax.Precision.HIGHEST,
        preferred_element_type=jnp.float32,
    )
    backward_in = jnp.dot(
        backward_weight, backward_parts, precision=lax.Precision.HIGHEST,
        preferred_element_type=jnp.float32,
    )
    returned = lax.all_to_all(
        jnp.concatenate(
            [forward_in.astype(jnp.bfloat16), backward_in.astype(jnp.bfloat16)], axis=1
        ),
        axis,
        0,
        0,
        tiled=True,
    )
    shape = (head_count, head_size, state_size)
    return (
        returned[:, :chunk].astype(jnp.float32).reshape(shape),
        returned[:, chunk:].astype(jnp.float32).reshape(shape),
    )


def block_pass(x_seq, dt_seq, b_seq, c_seq, forget_rate):
    row_count, head_count, head_size = x_seq.shape
    state_size = b_seq.shape[1]
    block_count = row_count // BLOCK
    x_blocks = x_seq.reshape(block_count, BLOCK, head_count, head_size)
    dt_blocks = dt_seq.reshape(head_count, block_count, BLOCK).transpose(1, 0, 2)
    b_blocks = b_seq.reshape(block_count, BLOCK, state_size)
    c_blocks = c_seq.reshape(block_count, BLOCK, state_size)
    cumulative = jnp.cumsum(-dt_blocks * forget_rate[None, :, None], axis=2)
    gram_matrix = jnp.einsum(
        "cqn,ckn->cqk", c_blocks, b_blocks, preferred_element_type=jnp.float32
    )
    symbol_offset = jnp.arange(BLOCK, dtype=jnp.int32)
    causal = symbol_offset[:, None] >= symbol_offset[None, :]
    spread = jnp.where(
        causal[None, None], cumulative[:, :, :, None] - cumulative[:, :, None, :], -jnp.inf
    )
    mixing = (gram_matrix[:, None] * jnp.exp(spread) * dt_blocks[:, :, None, :]).astype(
        jnp.bfloat16
    )
    intra_out = jnp.einsum(
        "chqk,ckhp->cqhp", mixing, x_blocks, preferred_element_type=jnp.float32
    )
    block_end = cumulative[:, :, -1]
    tail_weight = jnp.exp(block_end[:, :, None] - cumulative) * dt_blocks
    scaled_x = (x_blocks * tail_weight.transpose(0, 2, 1)[:, :, :, None]).astype(jnp.bfloat16)
    contrib = jnp.einsum(
        "ckhp,ckn->chpn", scaled_x, b_blocks, preferred_element_type=jnp.float32
    )
    decay_sum = jnp.zeros((head_count,), jnp.float32)
    running = jnp.zeros((head_count, head_size, state_size), jnp.float32)
    decay_sums = []
    runnings = []
    for c in range(block_count):
        decay_sums.append(decay_sum)
        runnings.append(running)
        running = jnp.exp(block_end[c])[:, None, None] * running + contrib[c]
        decay_sum = decay_sum + block_end[c]
    records = (intra_out, cumulative, jnp.stack(decay_sums), jnp.stack(runnings), c_blocks)
    return ((decay_sum, running), records)


def apply_state(records, incoming):
    intra_out, cumulative, decay_sums, runnings, c_blocks = records
    block_count = intra_out.shape[0]
    held_state = (
        jnp.exp(decay_sums)[:, :, None, None] * incoming[None] + runnings
    ).astype(jnp.bfloat16)
    state_out = jnp.einsum(
        "cqn,chpn->cqhp", c_blocks, held_state, preferred_element_type=jnp.float32
    )
    outputs = intra_out + state_out * jnp.exp(cumulative).transpose(0, 2, 1)[:, :, :, None]
    return outputs.reshape(block_count * BLOCK, outputs.shape[2] * outputs.shape[3])


def pool_combine(lo, hi):
    top = jnp.maximum(lo[0], hi[0])
    lo_scale = jnp.exp(lo[0] - top)
    hi_scale = jnp.exp(hi[0] - top)
    total = lo[1] * lo_scale + hi[1] * hi_scale
    summed = lo[2] * lo_scale[:, None] + hi[2] * hi_scale[:, None]
    return (top, total, summed)


def xor_exchange(value, axis, bit):
    count = lax.axis_size(axis)
    return lax.ppermute(value, axis, [(q, q ^ bit) for q in range(count)])


def reduce_pool(local, axis, scatter_rounds):
    count = lax.axis_size(axis)
    assert count & (count - 1) == 0
    place = lax.axis_index(axis)
    state = local
    bit = 1
    for unused_round in range(scatter_rounds):
        if bit >= count:
            break
        half = state[0].shape[0] // 2
        upper = (place & bit) != 0
        keep = jax.tree.map(lambda a: jnp.where(upper, a[half:], a[:half]), state)
        send = jax.tree.map(lambda a: jnp.where(upper, a[:half], a[half:]), state)
        received = xor_exchange((send[0], send[1], send[2].astype(jnp.bfloat16)), axis, bit)
        other = (received[0], received[1], received[2].astype(jnp.float32))
        state = pool_combine(keep, other)
        bit *= 2
    gather_bits = []
    while bit < count:
        sent = (state[0], state[1], state[2].astype(jnp.bfloat16))
        received = xor_exchange(sent, axis, bit)
        own = (sent[0], sent[1], sent[2].astype(jnp.float32))
        other = (received[0], received[1], received[2].astype(jnp.float32))
        is_low = (place & bit) == 0
        lo = jax.tree.map(lambda a, b: jnp.where(is_low, a, b), own, other)
        hi = jax.tree.map(lambda a, b: jnp.where(is_low, b, a), own, other)
        state = pool_combine(lo, hi)
        bit *= 2
    rows = (state[2] / state[1][:, None]).astype(jnp.bfloat16)
    bit = 1
    while bit * 2 <= count and len(gather_bits) < scatter_rounds:
        gather_bits.append(bit)
        bit *= 2
    for bit in reversed(gather_bits):
        received = xor_exchange(rows, axis, bit)
        upper = (place & bit) != 0
        rows = jnp.where(
            upper,
            jnp.concatenate([received, rows], axis=0),
            jnp.concatenate([rows, received], axis=0),
        )
    return rows


def all_to_all_pool(local, axis):
    count = lax.axis_size(axis)
    local_top, weight_sum, weighted_sum = local
    row_total, width = weighted_sum.shape
    rows = row_total // count
    stats = jnp.stack(split_wide(local_top) + split_wide(weight_sum), axis=0)
    stats = stats.reshape(4, count, rows).transpose(1, 0, 2).reshape(count, 4 * rows)
    pad = (-4 * rows) % 128
    packed = jnp.concatenate(
        [
            weighted_sum.astype(jnp.bfloat16).reshape(count, rows * width),
            jnp.pad(stats, ((0, 0), (0, pad))),
        ],
        axis=1,
    )
    moved = lax.all_to_all(packed, axis, 0, 0, tiled=True)
    parts = moved[:, : rows * width].reshape(count, rows, width).astype(jnp.float32)
    got = moved[:, rows * width : rows * width + 4 * rows].astype(jnp.float32)
    got = got.reshape(count, 4, rows)
    tops = got[:, 0] + got[:, 1]
    totals = got[:, 2] + got[:, 3]
    top = jnp.max(tops, axis=0)
    scale = jnp.exp(tops - top[None, :])
    total = jnp.sum(totals * scale, axis=0)
    summed = jnp.sum(parts * scale[:, :, None], axis=0)
    finished = (summed / total[:, None]).astype(jnp.bfloat16)
    spread_rows = jnp.broadcast_to(finished[None], (count, rows, width))
    gathered = lax.all_to_all(spread_rows, axis, 0, 0, tiled=True)
    return gathered.reshape(row_total, width)


def body(
    ssm_input,
    gate_input,
    state_proj,
    step_raw,
    decay_log,
    skip_gain,
    norm_gain,
    out_weight,
    latents,
    lengths,
):
    row_count = ssm_input.shape[1]
    inner_width = ssm_input.shape[2]
    head_count = decay_log.shape[1]
    head_size = inner_width // head_count
    state_size = state_proj.shape[2] // 4
    model_width = out_weight.shape[1]
    positions = lax.axis_index("seq") * row_count + jnp.arange(row_count, dtype=jnp.int32)
    is_valid = positions < lengths[0]
    step_size = jnp.where(is_valid[None, :], jax.nn.softplus(step_raw[0]), 0.0)
    decay_rates = jnp.exp(decay_log)
    flat_tokens = ssm_input[0]
    tokens = flat_tokens.reshape(row_count, head_count, head_size)
    projections = state_proj[0]
    forward_totals, forward_records = block_pass(
        tokens,
        step_size[:head_count],
        projections[:, :state_size],
        projections[:, state_size : 2 * state_size],
        decay_rates[0],
    )
    backward_totals, backward_records = block_pass(
        tokens[::-1],
        step_size[head_count:, ::-1],
        projections[::-1, 2 * state_size : 3 * state_size],
        projections[::-1, 3 * state_size :],
        decay_rates[1],
    )
    forward_in, backward_in = transposed_scans(forward_totals, backward_totals, "seq")
    forward_out = apply_state(forward_records, forward_in)
    backward_out = apply_state(backward_records, backward_in)[::-1]
    skip_wide = jnp.repeat(skip_gain, head_size)
    mixed_out = forward_out + backward_out + skip_wide[None, :] * flat_tokens.astype(jnp.float32)
    gated_out = mixed_out * jax.nn.silu(gate_input[0].astype(jnp.float32))
    squared = (gated_out * gated_out).reshape(row_count, head_count, head_size)
    mean_square = jnp.mean(squared, axis=2)
    inverse_scale = jnp.repeat(lax.rsqrt(mean_square + 1e-05), head_size, axis=1)
    normed = (gated_out * inverse_scale * norm_gain[None, :]).astype(jnp.bfloat16)
    projected = jnp.dot(
        normed,
        lax.all_gather(out_weight, "dp", axis=0, tiled=True),
        preferred_element_type=jnp.float32,
    )
    encoded = projected.astype(jnp.bfloat16)
    score_scale = 1.0 / math.sqrt(model_width)
    scores = (
        jnp.einsum("rd,sd->rs", latents, encoded, preferred_element_type=jnp.float32) * score_scale
    )
    local_top = jnp.max(jnp.where(is_valid[None, :], scores, -1e30), axis=1)
    prob_values = jnp.where(is_valid[None, :], jnp.exp(scores - local_top[:, None]), 0.0)
    weight_sum = jnp.sum(prob_values, axis=1)
    weighted_sum = jnp.dot(
        prob_values.astype(jnp.bfloat16), encoded, preferred_element_type=jnp.float32
    )
    pooled = all_to_all_pool((local_top, weight_sum, weighted_sum), "seq")
    return (encoded[None], pooled[None])


def solution(mesh):
    in_specs = (
        P("dp", "seq", None),
        P("dp", "seq", None),
        P("dp", "seq", None),
        P("dp", None, "seq"),
        P(),
        P(),
        P(),
        P("dp", None),
        P(),
        P("dp"),
    )
    out_specs = (P("dp", "seq", None), P("dp", None, None))
    return jax.shard_map(body, mesh=mesh, in_specs=in_specs, out_specs=out_specs, check_vma=False)
```

```python
import math

import jax
import jax.numpy as jnp
from jax import lax
from jax.sharding import PartitionSpec as P

BLOCK = 128


def chain_combine(earlier, later):
    return (
        earlier[0] + later[0],
        jnp.exp(later[0])[:, None, None] * earlier[1] + later[1],
    )


def exclusive_scans(parts, axis):
    count = lax.axis_size(axis)
    inclusive = [part for part, unused_item in parts]
    exclusive = [jax.tree.map(jnp.zeros_like, part) for part, unused_item in parts]
    rounds = max(1, (count - 1).bit_length())
    for k in range(rounds):
        shift = 1 << k
        if shift >= count:
            break
        received = []
        for i, (unused_item, reverse) in enumerate(parts):
            if reverse:
                perm = [(q, q - shift) for q in range(shift, count)]
            else:
                perm = [(q, q + shift) for q in range(count - shift)]
            sent = (inclusive[i][0], inclusive[i][1].astype(jnp.bfloat16))
            received.append(lax.ppermute(sent, axis, perm))
        received = lax.optimization_barrier(received)
        for i in range(len(parts)):
            got = (received[i][0], received[i][1].astype(jnp.float32))
            exclusive[i] = chain_combine(got, exclusive[i])
            if k + 1 < rounds:
                inclusive[i] = chain_combine(got, inclusive[i])
    return exclusive


def split_wide(values):
    rounded = lax.reduce_precision(values, exponent_bits=8, mantissa_bits=7)
    low = (values - rounded).astype(jnp.bfloat16)
    return rounded.astype(jnp.bfloat16), low


def transposed_scans(forward_totals, backward_totals, axis):
    count = lax.axis_size(axis)
    head_count, head_size, state_size = forward_totals[1].shape
    assert count % head_count == 0
    per_head = count // head_count
    chunk = head_size * state_size // per_head
    head_of = jnp.arange(count, dtype=jnp.int32) // per_head

    def pack(totals):
        flat = totals[1].astype(jnp.bfloat16).reshape(count, chunk)
        high, low = split_wide(totals[0][head_of])
        tail = jnp.zeros((count, 128), jnp.bfloat16).at[:, 0].set(high).at[:, 1].set(low)
        return jnp.concatenate([flat, tail], axis=1)

    width = chunk + 128
    got = lax.all_to_all(
        jnp.concatenate([pack(forward_totals), pack(backward_totals)], axis=1),
        axis,
        0,
        0,
        tiled=True,
    )

    def unpack(block):
        decay = block[:, chunk].astype(jnp.float32) + block[:, chunk + 1].astype(jnp.float32)
        return decay, block[:, :chunk].astype(jnp.float32)

    forward_decay, forward_parts = unpack(got[:, :width])
    backward_decay, backward_parts = unpack(got[:, width:])
    place = jnp.arange(count, dtype=jnp.int32)
    dest = place[:, None, None]
    source = place[None, :, None]
    between = place[None, None, :]
    forward_span = jnp.sum(
        jnp.where((source < between) & (between < dest), forward_decay[None, None, :], 0.0),
        axis=2,
    )
    forward_weight = jnp.where(place[None, :] < place[:, None], jnp.exp(forward_span), 0.0)
    backward_span = jnp.sum(
        jnp.where((dest < between) & (between < source), backward_decay[None, None, :], 0.0),
        axis=2,
    )
    backward_weight = jnp.where(place[None, :] > place[:, None], jnp.exp(backward_span), 0.0)
    forward_in = jnp.dot(
        forward_weight, forward_parts, precision=lax.Precision.HIGHEST,
        preferred_element_type=jnp.float32,
    )
    backward_in = jnp.dot(
        backward_weight, backward_parts, precision=lax.Precision.HIGHEST,
        preferred_element_type=jnp.float32,
    )
    returned = lax.all_to_all(
        jnp.concatenate(
            [forward_in.astype(jnp.bfloat16), backward_in.astype(jnp.bfloat16)], axis=1
        ),
        axis,
        0,
        0,
        tiled=True,
    )
    shape = (head_count, head_size, state_size)
    return (
        returned[:, :chunk].astype(jnp.float32).reshape(shape),
        returned[:, chunk:].astype(jnp.float32).reshape(shape),
    )


def block_pass(x_seq, dt_seq, b_seq, c_seq, forget_rate, reverse):
    row_count, head_count, head_size = x_seq.shape
    state_size = b_seq.shape[1]
    block_count = row_count // BLOCK
    x_blocks = x_seq.reshape(block_count, BLOCK, head_count, head_size)
    dt_blocks = dt_seq.reshape(head_count, block_count, BLOCK).transpose(1, 0, 2)
    b_blocks = b_seq.reshape(block_count, BLOCK, state_size)
    c_blocks = c_seq.reshape(block_count, BLOCK, state_size)
    cumulative = lax.cumsum(-dt_blocks * forget_rate[None, :, None], axis=2, reverse=reverse)
    gram_matrix = jnp.einsum(
        "cqn,ckn->cqk", c_blocks, b_blocks, preferred_element_type=jnp.float32
    )
    symbol_offset = jnp.arange(BLOCK, dtype=jnp.int32)
    if reverse:
        causal = symbol_offset[:, None] <= symbol_offset[None, :]
    else:
        causal = symbol_offset[:, None] >= symbol_offset[None, :]
    spread = jnp.where(
        causal[None, None], cumulative[:, :, :, None] - cumulative[:, :, None, :], -jnp.inf
    )
    mixing = (gram_matrix[:, None] * jnp.exp(spread) * dt_blocks[:, :, None, :]).astype(
        jnp.bfloat16
    )
    intra_out = jnp.einsum(
        "chqk,ckhp->cqhp", mixing, x_blocks, preferred_element_type=jnp.float32
    )
    block_end = cumulative[:, :, 0] if reverse else cumulative[:, :, -1]
    tail_weight = jnp.exp(block_end[:, :, None] - cumulative) * dt_blocks
    scaled_x = (x_blocks * tail_weight.transpose(0, 2, 1)[:, :, :, None]).astype(jnp.bfloat16)
    contrib = jnp.einsum(
        "ckhp,ckn->chpn", scaled_x, b_blocks, preferred_element_type=jnp.float32
    )
    decay_sum = jnp.zeros((head_count,), jnp.float32)
    running = jnp.zeros((head_count, head_size, state_size), jnp.float32)
    decay_sums = [None] * block_count
    runnings = [None] * block_count
    order = range(block_count - 1, -1, -1) if reverse else range(block_count)
    for c in order:
        decay_sums[c] = decay_sum
        runnings[c] = running
        running = jnp.exp(block_end[c])[:, None, None] * running + contrib[c]
        decay_sum = decay_sum + block_end[c]
    records = (intra_out, cumulative, jnp.stack(decay_sums), jnp.stack(runnings), c_blocks)
    return ((decay_sum, running), records)


def apply_state(records, incoming):
    intra_out, cumulative, decay_sums, runnings, c_blocks = records
    block_count = intra_out.shape[0]
    held_state = (
        jnp.exp(decay_sums)[:, :, None, None] * incoming[None] + runnings
    ).astype(jnp.bfloat16)
    state_out = jnp.einsum(
        "cqn,chpn->cqhp", c_blocks, held_state, preferred_element_type=jnp.float32
    )
    outputs = intra_out + state_out * jnp.exp(cumulative).transpose(0, 2, 1)[:, :, :, None]
    return outputs.reshape(block_count * BLOCK, outputs.shape[2] * outputs.shape[3])


def pool_combine(lo, hi):
    top = jnp.maximum(lo[0], hi[0])
    lo_scale = jnp.exp(lo[0] - top)
    hi_scale = jnp.exp(hi[0] - top)
    total = lo[1] * lo_scale + hi[1] * hi_scale
    summed = lo[2] * lo_scale[:, None] + hi[2] * hi_scale[:, None]
    return (top, total, summed)


def xor_exchange(value, axis, bit):
    count = lax.axis_size(axis)
    return lax.ppermute(value, axis, [(q, q ^ bit) for q in range(count)])


def reduce_pool(local, axis, scatter_rounds):
    count = lax.axis_size(axis)
    assert count & (count - 1) == 0
    place = lax.axis_index(axis)
    state = local
    bit = 1
    for unused_round in range(scatter_rounds):
        if bit >= count:
            break
        half = state[0].shape[0] // 2
        upper = (place & bit) != 0
        keep = jax.tree.map(lambda a: jnp.where(upper, a[half:], a[:half]), state)
        send = jax.tree.map(lambda a: jnp.where(upper, a[:half], a[half:]), state)
        received = xor_exchange((send[0], send[1], send[2].astype(jnp.bfloat16)), axis, bit)
        other = (received[0], received[1], received[2].astype(jnp.float32))
        state = pool_combine(keep, other)
        bit *= 2
    gather_bits = []
    while bit < count:
        sent = (state[0], state[1], state[2].astype(jnp.bfloat16))
        received = xor_exchange(sent, axis, bit)
        own = (sent[0], sent[1], sent[2].astype(jnp.float32))
        other = (received[0], received[1], received[2].astype(jnp.float32))
        is_low = (place & bit) == 0
        lo = jax.tree.map(lambda a, b: jnp.where(is_low, a, b), own, other)
        hi = jax.tree.map(lambda a, b: jnp.where(is_low, b, a), own, other)
        state = pool_combine(lo, hi)
        bit *= 2
    rows = (state[2] / state[1][:, None]).astype(jnp.bfloat16)
    bit = 1
    while bit * 2 <= count and len(gather_bits) < scatter_rounds:
        gather_bits.append(bit)
        bit *= 2
    for bit in reversed(gather_bits):
        received = xor_exchange(rows, axis, bit)
        upper = (place & bit) != 0
        rows = jnp.where(
            upper,
            jnp.concatenate([received, rows], axis=0),
            jnp.concatenate([rows, received], axis=0),
        )
    return rows


def all_to_all_pool(local, axis):
    count = lax.axis_size(axis)
    local_top, weight_sum, weighted_sum = local
    row_total, width = weighted_sum.shape
    rows = row_total // count
    stats = jnp.stack(split_wide(local_top) + split_wide(weight_sum), axis=0)
    stats = stats.reshape(4, count, rows).transpose(1, 0, 2).reshape(count, 4 * rows)
    pad = (-4 * rows) % 128
    packed = jnp.concatenate(
        [
            weighted_sum.astype(jnp.bfloat16).reshape(count, rows * width),
            jnp.pad(stats, ((0, 0), (0, pad))),
        ],
        axis=1,
    )
    moved = lax.all_to_all(packed, axis, 0, 0, tiled=True)
    parts = moved[:, : rows * width].reshape(count, rows, width).astype(jnp.float32)
    got = moved[:, rows * width : rows * width + 4 * rows].astype(jnp.float32)
    got = got.reshape(count, 4, rows)
    tops = got[:, 0] + got[:, 1]
    totals = got[:, 2] + got[:, 3]
    top = jnp.max(tops, axis=0)
    scale = jnp.exp(tops - top[None, :])
    total = jnp.sum(totals * scale, axis=0)
    summed = jnp.sum(parts * scale[:, :, None], axis=0)
    finished = (summed / total[:, None]).astype(jnp.bfloat16)
    spread_rows = jnp.broadcast_to(finished[None], (count, rows, width))
    gathered = lax.all_to_all(spread_rows, axis, 0, 0, tiled=True)
    return gathered.reshape(row_total, width)


def body(
    ssm_input,
    gate_input,
    state_proj,
    step_raw,
    decay_log,
    skip_gain,
    norm_gain,
    out_weight,
    latents,
    lengths,
):
    row_count = ssm_input.shape[1]
    inner_width = ssm_input.shape[2]
    head_count = decay_log.shape[1]
    head_size = inner_width // head_count
    state_size = state_proj.shape[2] // 4
    model_width = out_weight.shape[1]
    positions = lax.axis_index("seq") * row_count + jnp.arange(row_count, dtype=jnp.int32)
    is_valid = positions < lengths[0]
    step_size = jnp.where(is_valid[None, :], jax.nn.softplus(step_raw[0]), 0.0)
    decay_rates = jnp.exp(decay_log)
    flat_tokens = ssm_input[0]
    tokens = flat_tokens.reshape(row_count, head_count, head_size)
    projections = state_proj[0]
    forward_totals, forward_records = block_pass(
        tokens,
        step_size[:head_count],
        projections[:, :state_size],
        projections[:, state_size : 2 * state_size],
        decay_rates[0],
        False,
    )
    backward_totals, backward_records = block_pass(
        tokens,
        step_size[head_count:],
        projections[:, 2 * state_size : 3 * state_size],
        projections[:, 3 * state_size :],
        decay_rates[1],
        True,
    )
    forward_in, backward_in = transposed_scans(forward_totals, backward_totals, "seq")
    forward_out = apply_state(forward_records, forward_in)
    backward_out = apply_state(backward_records, backward_in)
    skip_wide = jnp.repeat(skip_gain, head_size)
    mixed_out = forward_out + backward_out + skip_wide[None, :] * flat_tokens.astype(jnp.float32)
    gated_out = mixed_out * jax.nn.silu(gate_input[0].astype(jnp.float32))
    squared = (gated_out * gated_out).reshape(row_count, head_count, head_size)
    mean_square = jnp.mean(squared, axis=2)
    inverse_scale = jnp.repeat(lax.rsqrt(mean_square + 1e-05), head_size, axis=1)
    normed = (gated_out * inverse_scale * norm_gain[None, :]).astype(jnp.bfloat16)
    projected = jnp.dot(
        normed,
        lax.all_gather(out_weight, "dp", axis=0, tiled=True),
        preferred_element_type=jnp.float32,
    )
    encoded = projected.astype(jnp.bfloat16)
    score_scale = 1.0 / math.sqrt(model_width)
    scores = (
        jnp.einsum("rd,sd->rs", latents, encoded, preferred_element_type=jnp.float32) * score_scale
    )
    local_top = jnp.max(jnp.where(is_valid[None, :], scores, -1e30), axis=1)
    prob_values = jnp.where(is_valid[None, :], jnp.exp(scores - local_top[:, None]), 0.0)
    weight_sum = jnp.sum(prob_values, axis=1)
    weighted_sum = jnp.dot(
        prob_values.astype(jnp.bfloat16), encoded, preferred_element_type=jnp.float32
    )
    pooled = all_to_all_pool((local_top, weight_sum, weighted_sum), "seq")
    return (encoded[None], pooled[None])


def solution(mesh):
    in_specs = (
        P("dp", "seq", None),
        P("dp", "seq", None),
        P("dp", "seq", None),
        P("dp", None, "seq"),
        P(),
        P(),
        P(),
        P("dp", None),
        P(),
        P("dp"),
    )
    out_specs = (P("dp", "seq", None), P("dp", None, None))
    return jax.shard_map(body, mesh=mesh, in_specs=in_specs, out_specs=out_specs, check_vma=False)
```

```python
import math

import jax
import jax.numpy as jnp
from jax import lax
from jax.sharding import PartitionSpec as P

BLOCK = 128


def chain_combine(earlier, later):
    return (
        earlier[0] + later[0],
        jnp.exp(later[0])[:, None, None] * earlier[1] + later[1],
    )


def exclusive_scans(parts, axis):
    count = lax.axis_size(axis)
    inclusive = [part for part, unused_item in parts]
    exclusive = [jax.tree.map(jnp.zeros_like, part) for part, unused_item in parts]
    rounds = max(1, (count - 1).bit_length())
    for k in range(rounds):
        shift = 1 << k
        if shift >= count:
            break
        received = []
        for i, (unused_item, reverse) in enumerate(parts):
            if reverse:
                perm = [(q, q - shift) for q in range(shift, count)]
            else:
                perm = [(q, q + shift) for q in range(count - shift)]
            sent = (inclusive[i][0], inclusive[i][1].astype(jnp.bfloat16))
            received.append(lax.ppermute(sent, axis, perm))
        received = lax.optimization_barrier(received)
        for i in range(len(parts)):
            got = (received[i][0], received[i][1].astype(jnp.float32))
            exclusive[i] = chain_combine(got, exclusive[i])
            if k + 1 < rounds:
                inclusive[i] = chain_combine(got, inclusive[i])
    return exclusive


def split_wide(values):
    rounded = lax.reduce_precision(values, exponent_bits=8, mantissa_bits=7)
    low = (values - rounded).astype(jnp.bfloat16)
    return rounded.astype(jnp.bfloat16), low


def transposed_scans(forward_totals, backward_totals, axis):
    count = lax.axis_size(axis)
    head_count, head_size, state_size = forward_totals[1].shape
    assert count % head_count == 0
    per_head = count // head_count
    rows = head_size // per_head
    head_of = jnp.arange(count, dtype=jnp.int32) // per_head
    decay_parts = split_wide(forward_totals[0][head_of]) + split_wide(backward_totals[0][head_of])
    decay_rows = jnp.zeros((count, 16, state_size), jnp.bfloat16)
    decay_rows = decay_rows.at[:, 0, :4].set(jnp.stack(decay_parts, axis=1))
    payload = jnp.concatenate(
        [
            forward_totals[1].astype(jnp.bfloat16).reshape(count, rows, state_size),
            backward_totals[1].astype(jnp.bfloat16).reshape(count, rows, state_size),
            decay_rows,
        ],
        axis=1,
    )
    got = lax.all_to_all(payload, axis, 0, 0, tiled=True)
    forward_parts = got[:, :rows].astype(jnp.float32)
    backward_parts = got[:, rows : 2 * rows].astype(jnp.float32)
    decays = got[:, 2 * rows, :4].astype(jnp.float32)
    forward_decay = decays[:, 0] + decays[:, 1]
    backward_decay = decays[:, 2] + decays[:, 3]
    place = jnp.arange(count, dtype=jnp.int32)
    dest = place[:, None, None]
    source = place[None, :, None]
    between = place[None, None, :]
    forward_span = jnp.sum(
        jnp.where((source < between) & (between < dest), forward_decay[None, None, :], 0.0),
        axis=2,
    )
    forward_weight = jnp.where(place[None, :] < place[:, None], jnp.exp(forward_span), 0.0)
    backward_span = jnp.sum(
        jnp.where((dest < between) & (between < source), backward_decay[None, None, :], 0.0),
        axis=2,
    )
    backward_weight = jnp.where(place[None, :] > place[:, None], jnp.exp(backward_span), 0.0)
    forward_in = jnp.einsum(
        "pq,qrn->prn", forward_weight, forward_parts, precision=lax.Precision.HIGHEST,
        preferred_element_type=jnp.float32,
    )
    backward_in = jnp.einsum(
        "pq,qrn->prn", backward_weight, backward_parts, precision=lax.Precision.HIGHEST,
        preferred_element_type=jnp.float32,
    )
    returned = lax.all_to_all(
        jnp.concatenate(
            [forward_in.astype(jnp.bfloat16), backward_in.astype(jnp.bfloat16)], axis=1
        ),
        axis,
        0,
        0,
        tiled=True,
    )
    shape = (head_count, head_size, state_size)
    return (
        returned[:, :rows].astype(jnp.float32).reshape(shape),
        returned[:, rows:].astype(jnp.float32).reshape(shape),
    )


def block_pass(x_seq, dt_seq, b_seq, c_seq, forget_rate, reverse):
    row_count, head_count, head_size = x_seq.shape
    state_size = b_seq.shape[1]
    block_count = row_count // BLOCK
    x_blocks = x_seq.reshape(block_count, BLOCK, head_count, head_size)
    dt_blocks = dt_seq.reshape(head_count, block_count, BLOCK).transpose(1, 0, 2)
    b_blocks = b_seq.reshape(block_count, BLOCK, state_size)
    c_blocks = c_seq.reshape(block_count, BLOCK, state_size)
    cumulative = lax.cumsum(-dt_blocks * forget_rate[None, :, None], axis=2, reverse=reverse)
    gram_matrix = jnp.einsum(
        "cqn,ckn->cqk", c_blocks, b_blocks, preferred_element_type=jnp.float32
    )
    symbol_offset = jnp.arange(BLOCK, dtype=jnp.int32)
    if reverse:
        causal = symbol_offset[:, None] <= symbol_offset[None, :]
    else:
        causal = symbol_offset[:, None] >= symbol_offset[None, :]
    spread = jnp.where(
        causal[None, None], cumulative[:, :, :, None] - cumulative[:, :, None, :], -jnp.inf
    )
    mixing = (gram_matrix[:, None] * jnp.exp(spread) * dt_blocks[:, :, None, :]).astype(
        jnp.bfloat16
    )
    intra_out = jnp.einsum(
        "chqk,ckhp->cqhp", mixing, x_blocks, preferred_element_type=jnp.float32
    )
    block_end = cumulative[:, :, 0] if reverse else cumulative[:, :, -1]
    tail_weight = jnp.exp(block_end[:, :, None] - cumulative) * dt_blocks
    scaled_x = (x_blocks * tail_weight.transpose(0, 2, 1)[:, :, :, None]).astype(jnp.bfloat16)
    contrib = jnp.einsum(
        "ckhp,ckn->chpn", scaled_x, b_blocks, preferred_element_type=jnp.float32
    )
    decay_sum = jnp.zeros((head_count,), jnp.float32)
    running = jnp.zeros((head_count, head_size, state_size), jnp.float32)
    decay_sums = [None] * block_count
    runnings = [None] * block_count
    order = range(block_count - 1, -1, -1) if reverse else range(block_count)
    for c in order:
        decay_sums[c] = decay_sum
        runnings[c] = running
        running = jnp.exp(block_end[c])[:, None, None] * running + contrib[c]
        decay_sum = decay_sum + block_end[c]
    records = (intra_out, cumulative, jnp.stack(decay_sums), jnp.stack(runnings), c_blocks)
    return ((decay_sum, running), records)


def apply_state(records, incoming):
    intra_out, cumulative, decay_sums, runnings, c_blocks = records
    block_count = intra_out.shape[0]
    held_state = (
        jnp.exp(decay_sums)[:, :, None, None] * incoming[None] + runnings
    ).astype(jnp.bfloat16)
    state_out = jnp.einsum(
        "cqn,chpn->cqhp", c_blocks, held_state, preferred_element_type=jnp.float32
    )
    outputs = intra_out + state_out * jnp.exp(cumulative).transpose(0, 2, 1)[:, :, :, None]
    return outputs.reshape(block_count * BLOCK, outputs.shape[2] * outputs.shape[3])


def pool_combine(lo, hi):
    top = jnp.maximum(lo[0], hi[0])
    lo_scale = jnp.exp(lo[0] - top)
    hi_scale = jnp.exp(hi[0] - top)
    total = lo[1] * lo_scale + hi[1] * hi_scale
    summed = lo[2] * lo_scale[:, None] + hi[2] * hi_scale[:, None]
    return (top, total, summed)


def xor_exchange(value, axis, bit):
    count = lax.axis_size(axis)
    return lax.ppermute(value, axis, [(q, q ^ bit) for q in range(count)])


def reduce_pool(local, axis, scatter_rounds):
    count = lax.axis_size(axis)
    assert count & (count - 1) == 0
    place = lax.axis_index(axis)
    state = local
    bit = 1
    for unused_round in range(scatter_rounds):
        if bit >= count:
            break
        half = state[0].shape[0] // 2
        upper = (place & bit) != 0
        keep = jax.tree.map(lambda a: jnp.where(upper, a[half:], a[:half]), state)
        send = jax.tree.map(lambda a: jnp.where(upper, a[:half], a[half:]), state)
        received = xor_exchange((send[0], send[1], send[2].astype(jnp.bfloat16)), axis, bit)
        other = (received[0], received[1], received[2].astype(jnp.float32))
        state = pool_combine(keep, other)
        bit *= 2
    gather_bits = []
    while bit < count:
        sent = (state[0], state[1], state[2].astype(jnp.bfloat16))
        received = xor_exchange(sent, axis, bit)
        own = (sent[0], sent[1], sent[2].astype(jnp.float32))
        other = (received[0], received[1], received[2].astype(jnp.float32))
        is_low = (place & bit) == 0
        lo = jax.tree.map(lambda a, b: jnp.where(is_low, a, b), own, other)
        hi = jax.tree.map(lambda a, b: jnp.where(is_low, b, a), own, other)
        state = pool_combine(lo, hi)
        bit *= 2
    rows = (state[2] / state[1][:, None]).astype(jnp.bfloat16)
    bit = 1
    while bit * 2 <= count and len(gather_bits) < scatter_rounds:
        gather_bits.append(bit)
        bit *= 2
    for bit in reversed(gather_bits):
        received = xor_exchange(rows, axis, bit)
        upper = (place & bit) != 0
        rows = jnp.where(
            upper,
            jnp.concatenate([received, rows], axis=0),
            jnp.concatenate([rows, received], axis=0),
        )
    return rows


def all_to_all_pool(local, axis):
    count = lax.axis_size(axis)
    local_top, weight_sum, weighted_sum = local
    row_total, width = weighted_sum.shape
    rows = row_total // count
    stats = jnp.stack(split_wide(local_top) + split_wide(weight_sum), axis=0)
    stats = stats.reshape(4, count, rows).transpose(1, 0, 2).reshape(count, 4 * rows)
    pad = (-4 * rows) % 128
    packed = jnp.concatenate(
        [
            weighted_sum.astype(jnp.bfloat16).reshape(count, rows * width),
            jnp.pad(stats, ((0, 0), (0, pad))),
        ],
        axis=1,
    )
    moved = lax.all_to_all(packed, axis, 0, 0, tiled=True)
    parts = moved[:, : rows * width].reshape(count, rows, width).astype(jnp.float32)
    got = moved[:, rows * width : rows * width + 4 * rows].astype(jnp.float32)
    got = got.reshape(count, 4, rows)
    tops = got[:, 0] + got[:, 1]
    totals = got[:, 2] + got[:, 3]
    top = jnp.max(tops, axis=0)
    scale = jnp.exp(tops - top[None, :])
    total = jnp.sum(totals * scale, axis=0)
    summed = jnp.sum(parts * scale[:, :, None], axis=0)
    finished = (summed / total[:, None]).astype(jnp.bfloat16)
    spread_rows = jnp.broadcast_to(finished[None], (count, rows, width))
    gathered = lax.all_to_all(spread_rows, axis, 0, 0, tiled=True)
    return gathered.reshape(row_total, width)


def body(
    ssm_input,
    gate_input,
    state_proj,
    step_raw,
    decay_log,
    skip_gain,
    norm_gain,
    out_weight,
    latents,
    lengths,
):
    row_count = ssm_input.shape[1]
    inner_width = ssm_input.shape[2]
    head_count = decay_log.shape[1]
    head_size = inner_width // head_count
    state_size = state_proj.shape[2] // 4
    model_width = out_weight.shape[1]
    positions = lax.axis_index("seq") * row_count + jnp.arange(row_count, dtype=jnp.int32)
    is_valid = positions < lengths[0]
    step_size = jnp.where(is_valid[None, :], jax.nn.softplus(step_raw[0]), 0.0)
    decay_rates = jnp.exp(decay_log)
    flat_tokens = ssm_input[0]
    tokens = flat_tokens.reshape(row_count, head_count, head_size)
    projections = state_proj[0]
    forward_totals, forward_records = block_pass(
        tokens,
        step_size[:head_count],
        projections[:, :state_size],
        projections[:, state_size : 2 * state_size],
        decay_rates[0],
        False,
    )
    backward_totals, backward_records = block_pass(
        tokens,
        step_size[head_count:],
        projections[:, 2 * state_size : 3 * state_size],
        projections[:, 3 * state_size :],
        decay_rates[1],
        True,
    )
    forward_in, backward_in = transposed_scans(forward_totals, backward_totals, "seq")
    forward_out = apply_state(forward_records, forward_in)
    backward_out = apply_state(backward_records, backward_in)
    skip_wide = jnp.repeat(skip_gain, head_size)
    mixed_out = forward_out + backward_out + skip_wide[None, :] * flat_tokens.astype(jnp.float32)
    gated_out = mixed_out * jax.nn.silu(gate_input[0].astype(jnp.float32))
    squared = (gated_out * gated_out).reshape(row_count, head_count, head_size)
    mean_square = jnp.mean(squared, axis=2)
    inverse_scale = jnp.repeat(lax.rsqrt(mean_square + 1e-05), head_size, axis=1)
    normed = (gated_out * inverse_scale * norm_gain[None, :]).astype(jnp.bfloat16)
    projected = jnp.dot(
        normed,
        lax.all_gather(out_weight, "dp", axis=0, tiled=True),
        preferred_element_type=jnp.float32,
    )
    encoded = projected.astype(jnp.bfloat16)
    score_scale = 1.0 / math.sqrt(model_width)
    scores = (
        jnp.einsum("rd,sd->rs", latents, encoded, preferred_element_type=jnp.float32) * score_scale
    )
    local_top = jnp.max(jnp.where(is_valid[None, :], scores, -1e30), axis=1)
    prob_values = jnp.where(is_valid[None, :], jnp.exp(scores - local_top[:, None]), 0.0)
    weight_sum = jnp.sum(prob_values, axis=1)
    weighted_sum = jnp.dot(
        prob_values.astype(jnp.bfloat16), encoded, preferred_element_type=jnp.float32
    )
    pooled = all_to_all_pool((local_top, weight_sum, weighted_sum), "seq")
    return (encoded[None], pooled[None])


def solution(mesh):
    in_specs = (
        P("dp", "seq", None),
        P("dp", "seq", None),
        P("dp", "seq", None),
        P("dp", None, "seq"),
        P(),
        P(),
        P(),
        P("dp", None),
        P(),
        P("dp"),
    )
    out_specs = (P("dp", "seq", None), P("dp", None, None))
    return jax.shard_map(body, mesh=mesh, in_specs=in_specs, out_specs=out_specs, check_vma=False)
```

```python
import math

import jax
import jax.numpy as jnp
from jax import lax
from jax.sharding import PartitionSpec as P

BLOCK = 128


def chain_combine(earlier, later):
    return (
        earlier[0] + later[0],
        jnp.exp(later[0])[:, None, None] * earlier[1] + later[1],
    )


def exclusive_scans(parts, axis):
    count = lax.axis_size(axis)
    inclusive = [part for part, unused_item in parts]
    exclusive = [jax.tree.map(jnp.zeros_like, part) for part, unused_item in parts]
    rounds = max(1, (count - 1).bit_length())
    for k in range(rounds):
        shift = 1 << k
        if shift >= count:
            break
        received = []
        for i, (unused_item, reverse) in enumerate(parts):
            if reverse:
                perm = [(q, q - shift) for q in range(shift, count)]
            else:
                perm = [(q, q + shift) for q in range(count - shift)]
            sent = (inclusive[i][0], inclusive[i][1].astype(jnp.bfloat16))
            received.append(lax.ppermute(sent, axis, perm))
        received = lax.optimization_barrier(received)
        for i in range(len(parts)):
            got = (received[i][0], received[i][1].astype(jnp.float32))
            exclusive[i] = chain_combine(got, exclusive[i])
            if k + 1 < rounds:
                inclusive[i] = chain_combine(got, inclusive[i])
    return exclusive


def split_wide(values):
    rounded = lax.reduce_precision(values, exponent_bits=8, mantissa_bits=7)
    low = (values - rounded).astype(jnp.bfloat16)
    return rounded.astype(jnp.bfloat16), low


def transposed_scans(forward_totals, backward_totals, axis, carried):
    count = lax.axis_size(axis)
    head_count, head_size, state_size = forward_totals[1].shape
    assert count % head_count == 0
    per_head = count // head_count
    rows = head_size // per_head
    head_of = jnp.arange(count, dtype=jnp.int32) // per_head
    decay_parts = split_wide(forward_totals[0][head_of]) + split_wide(backward_totals[0][head_of])
    decay_rows = jnp.zeros((count, 16, state_size), jnp.bfloat16)
    decay_rows = decay_rows.at[:, 0, :4].set(jnp.stack(decay_parts, axis=1))
    payload = jnp.concatenate(
        [
            forward_totals[1].astype(jnp.bfloat16).reshape(count, rows, state_size),
            backward_totals[1].astype(jnp.bfloat16).reshape(count, rows, state_size),
            decay_rows,
        ],
        axis=1,
    )
    payload, carried = lax.optimization_barrier((payload, carried))
    got = lax.all_to_all(payload, axis, 0, 0, tiled=True)
    forward_parts = got[:, :rows].astype(jnp.float32)
    backward_parts = got[:, rows : 2 * rows].astype(jnp.float32)
    decays = got[:, 2 * rows, :4].astype(jnp.float32)
    forward_decay = decays[:, 0] + decays[:, 1]
    backward_decay = decays[:, 2] + decays[:, 3]
    place = jnp.arange(count, dtype=jnp.int32)
    dest = place[:, None, None]
    source = place[None, :, None]
    between = place[None, None, :]
    forward_span = jnp.sum(
        jnp.where((source < between) & (between < dest), forward_decay[None, None, :], 0.0),
        axis=2,
    )
    forward_weight = jnp.where(place[None, :] < place[:, None], jnp.exp(forward_span), 0.0)
    backward_span = jnp.sum(
        jnp.where((dest < between) & (between < source), backward_decay[None, None, :], 0.0),
        axis=2,
    )
    backward_weight = jnp.where(place[None, :] > place[:, None], jnp.exp(backward_span), 0.0)
    forward_in = jnp.einsum(
        "pq,qrn->prn", forward_weight, forward_parts, precision=lax.Precision.HIGHEST,
        preferred_element_type=jnp.float32,
    )
    backward_in = jnp.einsum(
        "pq,qrn->prn", backward_weight, backward_parts, precision=lax.Precision.HIGHEST,
        preferred_element_type=jnp.float32,
    )
    returned = lax.all_to_all(
        jnp.concatenate(
            [forward_in.astype(jnp.bfloat16), backward_in.astype(jnp.bfloat16)], axis=1
        ),
        axis,
        0,
        0,
        tiled=True,
    )
    shape = (head_count, head_size, state_size)
    return (
        returned[:, :rows].astype(jnp.float32).reshape(shape),
        returned[:, rows:].astype(jnp.float32).reshape(shape),
        carried,
    )


def block_pass(x_seq, dt_seq, b_seq, c_seq, forget_rate, reverse):
    row_count, head_count, head_size = x_seq.shape
    state_size = b_seq.shape[1]
    block_count = row_count // BLOCK
    x_blocks = x_seq.reshape(block_count, BLOCK, head_count, head_size)
    dt_blocks = dt_seq.reshape(head_count, block_count, BLOCK).transpose(1, 0, 2)
    b_blocks = b_seq.reshape(block_count, BLOCK, state_size)
    c_blocks = c_seq.reshape(block_count, BLOCK, state_size)
    cumulative = lax.cumsum(-dt_blocks * forget_rate[None, :, None], axis=2, reverse=reverse)
    gram_matrix = jnp.einsum(
        "cqn,ckn->cqk", c_blocks, b_blocks, preferred_element_type=jnp.float32
    )
    symbol_offset = jnp.arange(BLOCK, dtype=jnp.int32)
    if reverse:
        causal = symbol_offset[:, None] <= symbol_offset[None, :]
    else:
        causal = symbol_offset[:, None] >= symbol_offset[None, :]
    spread = jnp.where(
        causal[None, None], cumulative[:, :, :, None] - cumulative[:, :, None, :], -jnp.inf
    )
    mixing = (gram_matrix[:, None] * jnp.exp(spread) * dt_blocks[:, :, None, :]).astype(
        jnp.bfloat16
    )
    intra_out = jnp.einsum(
        "chqk,ckhp->cqhp", mixing, x_blocks, preferred_element_type=jnp.float32
    )
    block_end = cumulative[:, :, 0] if reverse else cumulative[:, :, -1]
    tail_weight = jnp.exp(block_end[:, :, None] - cumulative) * dt_blocks
    scaled_x = (x_blocks * tail_weight.transpose(0, 2, 1)[:, :, :, None]).astype(jnp.bfloat16)
    contrib = jnp.einsum(
        "ckhp,ckn->chpn", scaled_x, b_blocks, preferred_element_type=jnp.float32
    )
    decay_sum = jnp.zeros((head_count,), jnp.float32)
    running = jnp.zeros((head_count, head_size, state_size), jnp.float32)
    decay_sums = [None] * block_count
    runnings = [None] * block_count
    order = range(block_count - 1, -1, -1) if reverse else range(block_count)
    for c in order:
        decay_sums[c] = decay_sum
        runnings[c] = running
        running = jnp.exp(block_end[c])[:, None, None] * running + contrib[c]
        decay_sum = decay_sum + block_end[c]
    records = (intra_out, cumulative, jnp.stack(decay_sums), jnp.stack(runnings), c_blocks)
    return ((decay_sum, running), records)


def apply_state(records, incoming):
    intra_out, cumulative, decay_sums, runnings, c_blocks = records
    block_count = intra_out.shape[0]
    held_state = (
        jnp.exp(decay_sums)[:, :, None, None] * incoming[None] + runnings
    ).astype(jnp.bfloat16)
    state_out = jnp.einsum(
        "cqn,chpn->cqhp", c_blocks, held_state, preferred_element_type=jnp.float32
    )
    outputs = intra_out + state_out * jnp.exp(cumulative).transpose(0, 2, 1)[:, :, :, None]
    return outputs.reshape(block_count * BLOCK, outputs.shape[2] * outputs.shape[3])


def pool_combine(lo, hi):
    top = jnp.maximum(lo[0], hi[0])
    lo_scale = jnp.exp(lo[0] - top)
    hi_scale = jnp.exp(hi[0] - top)
    total = lo[1] * lo_scale + hi[1] * hi_scale
    summed = lo[2] * lo_scale[:, None] + hi[2] * hi_scale[:, None]
    return (top, total, summed)


def xor_exchange(value, axis, bit):
    count = lax.axis_size(axis)
    return lax.ppermute(value, axis, [(q, q ^ bit) for q in range(count)])


def reduce_pool(local, axis, scatter_rounds):
    count = lax.axis_size(axis)
    assert count & (count - 1) == 0
    place = lax.axis_index(axis)
    state = local
    bit = 1
    for unused_round in range(scatter_rounds):
        if bit >= count:
            break
        half = state[0].shape[0] // 2
        upper = (place & bit) != 0
        keep = jax.tree.map(lambda a: jnp.where(upper, a[half:], a[:half]), state)
        send = jax.tree.map(lambda a: jnp.where(upper, a[:half], a[half:]), state)
        received = xor_exchange((send[0], send[1], send[2].astype(jnp.bfloat16)), axis, bit)
        other = (received[0], received[1], received[2].astype(jnp.float32))
        state = pool_combine(keep, other)
        bit *= 2
    gather_bits = []
    while bit < count:
        sent = (state[0], state[1], state[2].astype(jnp.bfloat16))
        received = xor_exchange(sent, axis, bit)
        own = (sent[0], sent[1], sent[2].astype(jnp.float32))
        other = (received[0], received[1], received[2].astype(jnp.float32))
        is_low = (place & bit) == 0
        lo = jax.tree.map(lambda a, b: jnp.where(is_low, a, b), own, other)
        hi = jax.tree.map(lambda a, b: jnp.where(is_low, b, a), own, other)
        state = pool_combine(lo, hi)
        bit *= 2
    rows = (state[2] / state[1][:, None]).astype(jnp.bfloat16)
    bit = 1
    while bit * 2 <= count and len(gather_bits) < scatter_rounds:
        gather_bits.append(bit)
        bit *= 2
    for bit in reversed(gather_bits):
        received = xor_exchange(rows, axis, bit)
        upper = (place & bit) != 0
        rows = jnp.where(
            upper,
            jnp.concatenate([received, rows], axis=0),
            jnp.concatenate([rows, received], axis=0),
        )
    return rows


def all_to_all_pool(local, axis):
    count = lax.axis_size(axis)
    local_top, weight_sum, weighted_sum = local
    row_total, width = weighted_sum.shape
    rows = row_total // count
    stats = jnp.stack(split_wide(local_top) + split_wide(weight_sum), axis=0)
    stats = stats.reshape(4, count, rows).transpose(1, 0, 2).reshape(count, 4 * rows)
    pad = (-4 * rows) % 128
    packed = jnp.concatenate(
        [
            weighted_sum.astype(jnp.bfloat16).reshape(count, rows * width),
            jnp.pad(stats, ((0, 0), (0, pad))),
        ],
        axis=1,
    )
    moved = lax.all_to_all(packed, axis, 0, 0, tiled=True)
    parts = moved[:, : rows * width].reshape(count, rows, width).astype(jnp.float32)
    got = moved[:, rows * width : rows * width + 4 * rows].astype(jnp.float32)
    got = got.reshape(count, 4, rows)
    tops = got[:, 0] + got[:, 1]
    totals = got[:, 2] + got[:, 3]
    top = jnp.max(tops, axis=0)
    scale = jnp.exp(tops - top[None, :])
    total = jnp.sum(totals * scale, axis=0)
    summed = jnp.sum(parts * scale[:, :, None], axis=0)
    finished = (summed / total[:, None]).astype(jnp.bfloat16)
    spread_rows = jnp.broadcast_to(finished[None], (count, rows, width))
    gathered = lax.all_to_all(spread_rows, axis, 0, 0, tiled=True)
    return gathered.reshape(row_total, width)


def body(
    ssm_input,
    gate_input,
    state_proj,
    step_raw,
    decay_log,
    skip_gain,
    norm_gain,
    out_weight,
    latents,
    lengths,
):
    row_count = ssm_input.shape[1]
    inner_width = ssm_input.shape[2]
    head_count = decay_log.shape[1]
    head_size = inner_width // head_count
    state_size = state_proj.shape[2] // 4
    model_width = out_weight.shape[1]
    positions = lax.axis_index("seq") * row_count + jnp.arange(row_count, dtype=jnp.int32)
    is_valid = positions < lengths[0]
    step_size = jnp.where(is_valid[None, :], jax.nn.softplus(step_raw[0]), 0.0)
    decay_rates = jnp.exp(decay_log)
    flat_tokens = ssm_input[0]
    tokens = flat_tokens.reshape(row_count, head_count, head_size)
    projections = state_proj[0]
    forward_totals, forward_records = block_pass(
        tokens,
        step_size[:head_count],
        projections[:, :state_size],
        projections[:, state_size : 2 * state_size],
        decay_rates[0],
        False,
    )
    backward_totals, backward_records = block_pass(
        tokens,
        step_size[head_count:],
        projections[:, 2 * state_size : 3 * state_size],
        projections[:, 3 * state_size :],
        decay_rates[1],
        True,
    )
    weight_groups = lax.axis_size("dp")
    full_weight = lax.all_to_all(
        jnp.broadcast_to(out_weight[None], (weight_groups,) + out_weight.shape),
        "dp",
        0,
        0,
        tiled=True,
    ).reshape(weight_groups * out_weight.shape[0], out_weight.shape[1])
    forward_in, backward_in, full_weight = transposed_scans(
        forward_totals, backward_totals, "seq", full_weight
    )
    forward_out = apply_state(forward_records, forward_in)
    backward_out = apply_state(backward_records, backward_in)
    skip_wide = jnp.repeat(skip_gain, head_size)
    mixed_out = forward_out + backward_out + skip_wide[None, :] * flat_tokens.astype(jnp.float32)
    gated_out = mixed_out * jax.nn.silu(gate_input[0].astype(jnp.float32))
    squared = (gated_out * gated_out).reshape(row_count, head_count, head_size)
    mean_square = jnp.mean(squared, axis=2)
    inverse_scale = jnp.repeat(lax.rsqrt(mean_square + 1e-05), head_size, axis=1)
    normed = (gated_out * inverse_scale * norm_gain[None, :]).astype(jnp.bfloat16)
    projected = jnp.dot(normed, full_weight, preferred_element_type=jnp.float32)
    encoded = projected.astype(jnp.bfloat16)
    score_scale = 1.0 / math.sqrt(model_width)
    scores = (
        jnp.einsum("rd,sd->rs", latents, encoded, preferred_element_type=jnp.float32) * score_scale
    )
    local_top = jnp.max(jnp.where(is_valid[None, :], scores, -1e30), axis=1)
    prob_values = jnp.where(is_valid[None, :], jnp.exp(scores - local_top[:, None]), 0.0)
    weight_sum = jnp.sum(prob_values, axis=1)
    weighted_sum = jnp.dot(
        prob_values.astype(jnp.bfloat16), encoded, preferred_element_type=jnp.float32
    )
    pooled = all_to_all_pool((local_top, weight_sum, weighted_sum), "seq")
    return (encoded[None], pooled[None])


def solution(mesh):
    in_specs = (
        P("dp", "seq", None),
        P("dp", "seq", None),
        P("dp", "seq", None),
        P("dp", None, "seq"),
        P(),
        P(),
        P(),
        P("dp", None),
        P(),
        P("dp"),
    )
    out_specs = (P("dp", "seq", None), P("dp", None, None))
    return jax.shard_map(body, mesh=mesh, in_specs=in_specs, out_specs=out_specs, check_vma=False)
```

```python
import math

import jax
import jax.numpy as jnp
from jax import lax
from jax.sharding import PartitionSpec as P

BLOCK = 128


def chain_combine(earlier, later):
    return (
        earlier[0] + later[0],
        jnp.exp(later[0])[:, None, None] * earlier[1] + later[1],
    )


def exclusive_scans(parts, axis):
    count = lax.axis_size(axis)
    inclusive = [part for part, unused_item in parts]
    exclusive = [jax.tree.map(jnp.zeros_like, part) for part, unused_item in parts]
    rounds = max(1, (count - 1).bit_length())
    for k in range(rounds):
        shift = 1 << k
        if shift >= count:
            break
        received = []
        for i, (unused_item, reverse) in enumerate(parts):
            if reverse:
                perm = [(q, q - shift) for q in range(shift, count)]
            else:
                perm = [(q, q + shift) for q in range(count - shift)]
            sent = (inclusive[i][0], inclusive[i][1].astype(jnp.bfloat16))
            received.append(lax.ppermute(sent, axis, perm))
        received = lax.optimization_barrier(received)
        for i in range(len(parts)):
            got = (received[i][0], received[i][1].astype(jnp.float32))
            exclusive[i] = chain_combine(got, exclusive[i])
            if k + 1 < rounds:
                inclusive[i] = chain_combine(got, inclusive[i])
    return exclusive


def split_wide(values):
    rounded = lax.reduce_precision(values, exponent_bits=8, mantissa_bits=7)
    low = (values - rounded).astype(jnp.bfloat16)
    return rounded.astype(jnp.bfloat16), low


def transposed_scans(forward_totals, backward_totals, axis, carried):
    count = lax.axis_size(axis)
    head_count, head_size, state_size = forward_totals[1].shape
    assert count % head_count == 0
    per_head = count // head_count
    rows = head_size // per_head
    head_of = jnp.arange(count, dtype=jnp.int32) // per_head
    decay_parts = split_wide(forward_totals[0][head_of]) + split_wide(backward_totals[0][head_of])
    decay_rows = jnp.zeros((count, 16, state_size), jnp.bfloat16)
    decay_rows = decay_rows.at[:, 0, :4].set(jnp.stack(decay_parts, axis=1))
    payload = jnp.concatenate(
        [
            forward_totals[1].astype(jnp.bfloat16).reshape(count, rows, state_size),
            backward_totals[1].astype(jnp.bfloat16).reshape(count, rows, state_size),
            decay_rows,
        ],
        axis=1,
    )
    payload, carried = lax.optimization_barrier((payload, carried))
    got = lax.all_to_all(payload, axis, 0, 0, tiled=True)
    forward_parts = got[:, :rows].astype(jnp.float32)
    backward_parts = got[:, rows : 2 * rows].astype(jnp.float32)
    decays = got[:, 2 * rows, :4].astype(jnp.float32)
    forward_decay = decays[:, 0] + decays[:, 1]
    backward_decay = decays[:, 2] + decays[:, 3]
    place = jnp.arange(count, dtype=jnp.int32)
    dest = place[:, None, None]
    source = place[None, :, None]
    between = place[None, None, :]
    forward_span = jnp.sum(
        jnp.where((source < between) & (between < dest), forward_decay[None, None, :], 0.0),
        axis=2,
    )
    forward_weight = jnp.where(place[None, :] < place[:, None], jnp.exp(forward_span), 0.0)
    backward_span = jnp.sum(
        jnp.where((dest < between) & (between < source), backward_decay[None, None, :], 0.0),
        axis=2,
    )
    backward_weight = jnp.where(place[None, :] > place[:, None], jnp.exp(backward_span), 0.0)
    forward_in = jnp.einsum(
        "pq,qrn->prn", forward_weight, forward_parts, precision=lax.Precision.HIGHEST,
        preferred_element_type=jnp.float32,
    )
    backward_in = jnp.einsum(
        "pq,qrn->prn", backward_weight, backward_parts, precision=lax.Precision.HIGHEST,
        preferred_element_type=jnp.float32,
    )
    returned = lax.all_to_all(
        jnp.concatenate(
            [forward_in.astype(jnp.bfloat16), backward_in.astype(jnp.bfloat16)], axis=1
        ),
        axis,
        0,
        0,
        tiled=True,
    )
    shape = (head_count, head_size, state_size)
    return (
        returned[:, :rows].astype(jnp.float32).reshape(shape),
        returned[:, rows:].astype(jnp.float32).reshape(shape),
        carried,
    )


def block_pass(x_seq, dt_seq, b_seq, c_seq, forget_rate, reverse):
    row_count, head_count, head_size = x_seq.shape
    state_size = b_seq.shape[1]
    block_count = row_count // BLOCK
    x_blocks = x_seq.reshape(block_count, BLOCK, head_count, head_size)
    dt_blocks = dt_seq.reshape(head_count, block_count, BLOCK).transpose(1, 0, 2)
    b_blocks = b_seq.reshape(block_count, BLOCK, state_size)
    c_blocks = c_seq.reshape(block_count, BLOCK, state_size)
    cumulative = lax.cumsum(-dt_blocks * forget_rate[None, :, None], axis=2, reverse=reverse)
    gram_matrix = jnp.einsum(
        "cqn,ckn->cqk", c_blocks, b_blocks, preferred_element_type=jnp.float32
    )
    symbol_offset = jnp.arange(BLOCK, dtype=jnp.int32)
    if reverse:
        causal = symbol_offset[:, None] <= symbol_offset[None, :]
    else:
        causal = symbol_offset[:, None] >= symbol_offset[None, :]
    spread = jnp.where(
        causal[None, None], cumulative[:, :, :, None] - cumulative[:, :, None, :], -jnp.inf
    )
    mixing = (gram_matrix[:, None] * jnp.exp(spread) * dt_blocks[:, :, None, :]).astype(
        jnp.bfloat16
    )
    intra_out = jnp.einsum(
        "chqk,ckhp->cqhp", mixing, x_blocks, preferred_element_type=jnp.float32
    )
    block_end = cumulative[:, :, 0] if reverse else cumulative[:, :, -1]
    tail_weight = jnp.exp(block_end[:, :, None] - cumulative) * dt_blocks
    scaled_x = (x_blocks * tail_weight.transpose(0, 2, 1)[:, :, :, None]).astype(jnp.bfloat16)
    contrib = jnp.einsum(
        "ckhp,ckn->chpn", scaled_x, b_blocks, preferred_element_type=jnp.float32
    )
    decay_sum = jnp.zeros((head_count,), jnp.float32)
    running = jnp.zeros((head_count, head_size, state_size), jnp.float32)
    decay_sums = [None] * block_count
    runnings = [None] * block_count
    order = range(block_count - 1, -1, -1) if reverse else range(block_count)
    for c in order:
        decay_sums[c] = decay_sum
        runnings[c] = running
        running = jnp.exp(block_end[c])[:, None, None] * running + contrib[c]
        decay_sum = decay_sum + block_end[c]
    records = (intra_out, cumulative, jnp.stack(decay_sums), jnp.stack(runnings), c_blocks)
    return ((decay_sum, running), records)


def apply_state(records, incoming):
    intra_out, cumulative, decay_sums, runnings, c_blocks = records
    block_count = intra_out.shape[0]
    held_state = (
        jnp.exp(decay_sums)[:, :, None, None] * incoming[None] + runnings
    ).astype(jnp.bfloat16)
    state_out = jnp.einsum(
        "cqn,chpn->cqhp", c_blocks, held_state, preferred_element_type=jnp.float32
    )
    outputs = intra_out + state_out * jnp.exp(cumulative).transpose(0, 2, 1)[:, :, :, None]
    return outputs.reshape(block_count * BLOCK, outputs.shape[2] * outputs.shape[3])


def pool_combine(lo, hi):
    top = jnp.maximum(lo[0], hi[0])
    lo_scale = jnp.exp(lo[0] - top)
    hi_scale = jnp.exp(hi[0] - top)
    total = lo[1] * lo_scale + hi[1] * hi_scale
    summed = lo[2] * lo_scale[:, None] + hi[2] * hi_scale[:, None]
    return (top, total, summed)


def xor_exchange(value, axis, bit):
    count = lax.axis_size(axis)
    return lax.ppermute(value, axis, [(q, q ^ bit) for q in range(count)])


def reduce_pool(local, axis, scatter_rounds):
    count = lax.axis_size(axis)
    assert count & (count - 1) == 0
    place = lax.axis_index(axis)
    state = local
    bit = 1
    for unused_round in range(scatter_rounds):
        if bit >= count:
            break
        half = state[0].shape[0] // 2
        upper = (place & bit) != 0
        keep = jax.tree.map(lambda a: jnp.where(upper, a[half:], a[:half]), state)
        send = jax.tree.map(lambda a: jnp.where(upper, a[:half], a[half:]), state)
        received = xor_exchange((send[0], send[1], send[2].astype(jnp.bfloat16)), axis, bit)
        other = (received[0], received[1], received[2].astype(jnp.float32))
        state = pool_combine(keep, other)
        bit *= 2
    gather_bits = []
    while bit < count:
        sent = (state[0], state[1], state[2].astype(jnp.bfloat16))
        received = xor_exchange(sent, axis, bit)
        own = (sent[0], sent[1], sent[2].astype(jnp.float32))
        other = (received[0], received[1], received[2].astype(jnp.float32))
        is_low = (place & bit) == 0
        lo = jax.tree.map(lambda a, b: jnp.where(is_low, a, b), own, other)
        hi = jax.tree.map(lambda a, b: jnp.where(is_low, b, a), own, other)
        state = pool_combine(lo, hi)
        bit *= 2
    rows = (state[2] / state[1][:, None]).astype(jnp.bfloat16)
    bit = 1
    while bit * 2 <= count and len(gather_bits) < scatter_rounds:
        gather_bits.append(bit)
        bit *= 2
    for bit in reversed(gather_bits):
        received = xor_exchange(rows, axis, bit)
        upper = (place & bit) != 0
        rows = jnp.where(
            upper,
            jnp.concatenate([received, rows], axis=0),
            jnp.concatenate([rows, received], axis=0),
        )
    return rows


def all_to_all_pool(local, axis):
    count = lax.axis_size(axis)
    local_top, weight_sum, weighted_sum = local
    row_total, width = weighted_sum.shape
    rows = row_total // count
    stats = jnp.stack(split_wide(local_top) + split_wide(weight_sum), axis=0)
    stats = stats.reshape(4, count, rows).transpose(1, 2, 0)
    packed = jnp.concatenate(
        [
            weighted_sum.astype(jnp.bfloat16).reshape(count, rows, width),
            jnp.pad(stats, ((0, 0), (0, 0), (0, 124))),
        ],
        axis=2,
    )
    moved = lax.all_to_all(packed, axis, 0, 0, tiled=True)
    parts = moved[:, :, :width].astype(jnp.float32)
    got = moved[:, :, width : width + 4].astype(jnp.float32)
    tops = got[:, :, 0] + got[:, :, 1]
    totals = got[:, :, 2] + got[:, :, 3]
    top = jnp.max(tops, axis=0)
    scale = jnp.exp(tops - top[None, :])
    total = jnp.sum(totals * scale, axis=0)
    summed = jnp.sum(parts * scale[:, :, None], axis=0)
    finished = (summed / total[:, None]).astype(jnp.bfloat16)
    spread_rows = jnp.broadcast_to(finished[None], (count, rows, width))
    gathered = lax.all_to_all(spread_rows, axis, 0, 0, tiled=True)
    return gathered.reshape(row_total, width)


def body(
    ssm_input,
    gate_input,
    state_proj,
    step_raw,
    decay_log,
    skip_gain,
    norm_gain,
    out_weight,
    latents,
    lengths,
):
    row_count = ssm_input.shape[1]
    inner_width = ssm_input.shape[2]
    head_count = decay_log.shape[1]
    head_size = inner_width // head_count
    state_size = state_proj.shape[2] // 4
    model_width = out_weight.shape[1]
    positions = lax.axis_index("seq") * row_count + jnp.arange(row_count, dtype=jnp.int32)
    is_valid = positions < lengths[0]
    step_size = jnp.where(is_valid[None, :], jax.nn.softplus(step_raw[0]), 0.0)
    decay_rates = jnp.exp(decay_log)
    flat_tokens = ssm_input[0]
    tokens = flat_tokens.reshape(row_count, head_count, head_size)
    projections = state_proj[0]
    forward_totals, forward_records = block_pass(
        tokens,
        step_size[:head_count],
        projections[:, :state_size],
        projections[:, state_size : 2 * state_size],
        decay_rates[0],
        False,
    )
    backward_totals, backward_records = block_pass(
        tokens,
        step_size[head_count:],
        projections[:, 2 * state_size : 3 * state_size],
        projections[:, 3 * state_size :],
        decay_rates[1],
        True,
    )
    weight_groups = lax.axis_size("dp")
    full_weight = lax.all_to_all(
        jnp.broadcast_to(out_weight[None], (weight_groups,) + out_weight.shape),
        "dp",
        0,
        0,
        tiled=True,
    ).reshape(weight_groups * out_weight.shape[0], out_weight.shape[1])
    forward_in, backward_in, full_weight = transposed_scans(
        forward_totals, backward_totals, "seq", full_weight
    )
    forward_out = apply_state(forward_records, forward_in)
    backward_out = apply_state(backward_records, backward_in)
    skip_wide = jnp.repeat(skip_gain, head_size)
    mixed_out = forward_out + backward_out + skip_wide[None, :] * flat_tokens.astype(jnp.float32)
    gated_out = mixed_out * jax.nn.silu(gate_input[0].astype(jnp.float32))
    squared = (gated_out * gated_out).reshape(row_count, head_count, head_size)
    mean_square = jnp.mean(squared, axis=2)
    inverse_scale = jnp.repeat(lax.rsqrt(mean_square + 1e-05), head_size, axis=1)
    normed = (gated_out * inverse_scale * norm_gain[None, :]).astype(jnp.bfloat16)
    projected = jnp.dot(normed, full_weight, preferred_element_type=jnp.float32)
    encoded = projected.astype(jnp.bfloat16)
    score_scale = 1.0 / math.sqrt(model_width)
    scores = (
        jnp.einsum("rd,sd->rs", latents, encoded, preferred_element_type=jnp.float32) * score_scale
    )
    local_top = jnp.max(jnp.where(is_valid[None, :], scores, -1e30), axis=1)
    prob_values = jnp.where(is_valid[None, :], jnp.exp(scores - local_top[:, None]), 0.0)
    weight_sum = jnp.sum(prob_values, axis=1)
    weighted_sum = jnp.dot(
        prob_values.astype(jnp.bfloat16), encoded, preferred_element_type=jnp.float32
    )
    pooled = all_to_all_pool((local_top, weight_sum, weighted_sum), "seq")
    return (encoded[None], pooled[None])


def solution(mesh):
    in_specs = (
        P("dp", "seq", None),
        P("dp", "seq", None),
        P("dp", "seq", None),
        P("dp", None, "seq"),
        P(),
        P(),
        P(),
        P("dp", None),
        P(),
        P("dp"),
    )
    out_specs = (P("dp", "seq", None), P("dp", None, None))
    return jax.shard_map(body, mesh=mesh, in_specs=in_specs, out_specs=out_specs, check_vma=False)
```

```python
import math

import jax
import jax.numpy as jnp
from jax import lax
from jax.sharding import PartitionSpec as P

BLOCK = 128


def chain_combine(earlier, later):
    return (
        earlier[0] + later[0],
        jnp.exp(later[0])[:, None, None] * earlier[1] + later[1],
    )


def exclusive_scans(parts, axis):
    count = lax.axis_size(axis)
    inclusive = [part for part, unused_item in parts]
    exclusive = [jax.tree.map(jnp.zeros_like, part) for part, unused_item in parts]
    rounds = max(1, (count - 1).bit_length())
    for k in range(rounds):
        shift = 1 << k
        if shift >= count:
            break
        received = []
        for i, (unused_item, reverse) in enumerate(parts):
            if reverse:
                perm = [(q, q - shift) for q in range(shift, count)]
            else:
                perm = [(q, q + shift) for q in range(count - shift)]
            sent = (inclusive[i][0], inclusive[i][1].astype(jnp.bfloat16))
            received.append(lax.ppermute(sent, axis, perm))
        received = lax.optimization_barrier(received)
        for i in range(len(parts)):
            got = (received[i][0], received[i][1].astype(jnp.float32))
            exclusive[i] = chain_combine(got, exclusive[i])
            if k + 1 < rounds:
                inclusive[i] = chain_combine(got, inclusive[i])
    return exclusive


def split_wide(values):
    rounded = lax.reduce_precision(values, exponent_bits=8, mantissa_bits=7)
    low = (values - rounded).astype(jnp.bfloat16)
    return rounded.astype(jnp.bfloat16), low


def transposed_scans(forward_totals, backward_totals, axis, carried):
    count = lax.axis_size(axis)
    head_count, head_size, state_size = forward_totals[1].shape
    assert count % head_count == 0
    per_head = count // head_count
    rows = head_size // per_head
    head_of = jnp.arange(count, dtype=jnp.int32) // per_head
    decay_parts = split_wide(forward_totals[0][head_of]) + split_wide(backward_totals[0][head_of])
    decay_rows = jnp.zeros((count, 16, state_size), jnp.bfloat16)
    decay_rows = decay_rows.at[:, 0, :4].set(jnp.stack(decay_parts, axis=1))
    payload = jnp.concatenate(
        [
            forward_totals[1].astype(jnp.bfloat16).reshape(count, rows, state_size),
            backward_totals[1].astype(jnp.bfloat16).reshape(count, rows, state_size),
            decay_rows,
        ],
        axis=1,
    )
    payload, carried = lax.optimization_barrier((payload, carried))
    got = lax.all_to_all(payload, axis, 0, 0, tiled=True)
    forward_parts = got[:, :rows].astype(jnp.float32)
    backward_parts = got[:, rows : 2 * rows].astype(jnp.float32)
    decays = got[:, 2 * rows, :4].astype(jnp.float32)
    forward_decay = decays[:, 0] + decays[:, 1]
    backward_decay = decays[:, 2] + decays[:, 3]
    place = jnp.arange(count, dtype=jnp.int32)
    dest = place[:, None, None]
    source = place[None, :, None]
    between = place[None, None, :]
    forward_span = jnp.sum(
        jnp.where((source < between) & (between < dest), forward_decay[None, None, :], 0.0),
        axis=2,
    )
    forward_weight = jnp.where(place[None, :] < place[:, None], jnp.exp(forward_span), 0.0)
    backward_span = jnp.sum(
        jnp.where((dest < between) & (between < source), backward_decay[None, None, :], 0.0),
        axis=2,
    )
    backward_weight = jnp.where(place[None, :] > place[:, None], jnp.exp(backward_span), 0.0)
    forward_in = jnp.einsum(
        "pq,qrn->prn", forward_weight, forward_parts, precision=lax.Precision.HIGH,
        preferred_element_type=jnp.float32,
    )
    backward_in = jnp.einsum(
        "pq,qrn->prn", backward_weight, backward_parts, precision=lax.Precision.HIGH,
        preferred_element_type=jnp.float32,
    )
    returned = lax.all_to_all(
        jnp.concatenate(
            [forward_in.astype(jnp.bfloat16), backward_in.astype(jnp.bfloat16)], axis=1
        ),
        axis,
        0,
        0,
        tiled=True,
    )
    shape = (head_count, head_size, state_size)
    return (
        returned[:, :rows].astype(jnp.float32).reshape(shape),
        returned[:, rows:].astype(jnp.float32).reshape(shape),
        carried,
    )


def block_pass(x_seq, dt_seq, b_seq, c_seq, forget_rate, reverse):
    row_count, head_count, head_size = x_seq.shape
    state_size = b_seq.shape[1]
    block_count = row_count // BLOCK
    x_blocks = x_seq.reshape(block_count, BLOCK, head_count, head_size)
    dt_blocks = dt_seq.reshape(head_count, block_count, BLOCK).transpose(1, 0, 2)
    b_blocks = b_seq.reshape(block_count, BLOCK, state_size)
    c_blocks = c_seq.reshape(block_count, BLOCK, state_size)
    cumulative = lax.cumsum(-dt_blocks * forget_rate[None, :, None], axis=2, reverse=reverse)
    gram_matrix = jnp.einsum(
        "cqn,ckn->cqk", c_blocks, b_blocks, preferred_element_type=jnp.float32
    )
    symbol_offset = jnp.arange(BLOCK, dtype=jnp.int32)
    if reverse:
        causal = symbol_offset[:, None] <= symbol_offset[None, :]
    else:
        causal = symbol_offset[:, None] >= symbol_offset[None, :]
    spread = jnp.where(
        causal[None, None], cumulative[:, :, :, None] - cumulative[:, :, None, :], -jnp.inf
    )
    mixing = (gram_matrix[:, None] * jnp.exp(spread) * dt_blocks[:, :, None, :]).astype(
        jnp.bfloat16
    )
    intra_out = jnp.einsum(
        "chqk,ckhp->cqhp", mixing, x_blocks, preferred_element_type=jnp.float32
    )
    block_end = cumulative[:, :, 0] if reverse else cumulative[:, :, -1]
    tail_weight = jnp.exp(block_end[:, :, None] - cumulative) * dt_blocks
    scaled_x = (x_blocks * tail_weight.transpose(0, 2, 1)[:, :, :, None]).astype(jnp.bfloat16)
    contrib = jnp.einsum(
        "ckhp,ckn->chpn", scaled_x, b_blocks, preferred_element_type=jnp.float32
    )
    decay_sum = jnp.zeros((head_count,), jnp.float32)
    running = jnp.zeros((head_count, head_size, state_size), jnp.float32)
    decay_sums = [None] * block_count
    runnings = [None] * block_count
    order = range(block_count - 1, -1, -1) if reverse else range(block_count)
    for c in order:
        decay_sums[c] = decay_sum
        runnings[c] = running
        running = jnp.exp(block_end[c])[:, None, None] * running + contrib[c]
        decay_sum = decay_sum + block_end[c]
    records = (intra_out, cumulative, jnp.stack(decay_sums), jnp.stack(runnings), c_blocks)
    return ((decay_sum, running), records)


def apply_state(records, incoming):
    intra_out, cumulative, decay_sums, runnings, c_blocks = records
    block_count = intra_out.shape[0]
    held_state = (
        jnp.exp(decay_sums)[:, :, None, None] * incoming[None] + runnings
    ).astype(jnp.bfloat16)
    state_out = jnp.einsum(
        "cqn,chpn->cqhp", c_blocks, held_state, preferred_element_type=jnp.float32
    )
    outputs = intra_out + state_out * jnp.exp(cumulative).transpose(0, 2, 1)[:, :, :, None]
    return outputs.reshape(block_count * BLOCK, outputs.shape[2] * outputs.shape[3])


def pool_combine(lo, hi):
    top = jnp.maximum(lo[0], hi[0])
    lo_scale = jnp.exp(lo[0] - top)
    hi_scale = jnp.exp(hi[0] - top)
    total = lo[1] * lo_scale + hi[1] * hi_scale
    summed = lo[2] * lo_scale[:, None] + hi[2] * hi_scale[:, None]
    return (top, total, summed)


def xor_exchange(value, axis, bit):
    count = lax.axis_size(axis)
    return lax.ppermute(value, axis, [(q, q ^ bit) for q in range(count)])


def reduce_pool(local, axis, scatter_rounds):
    count = lax.axis_size(axis)
    assert count & (count - 1) == 0
    place = lax.axis_index(axis)
    state = local
    bit = 1
    for unused_round in range(scatter_rounds):
        if bit >= count:
            break
        half = state[0].shape[0] // 2
        upper = (place & bit) != 0
        keep = jax.tree.map(lambda a: jnp.where(upper, a[half:], a[:half]), state)
        send = jax.tree.map(lambda a: jnp.where(upper, a[:half], a[half:]), state)
        received = xor_exchange((send[0], send[1], send[2].astype(jnp.bfloat16)), axis, bit)
        other = (received[0], received[1], received[2].astype(jnp.float32))
        state = pool_combine(keep, other)
        bit *= 2
    gather_bits = []
    while bit < count:
        sent = (state[0], state[1], state[2].astype(jnp.bfloat16))
        received = xor_exchange(sent, axis, bit)
        own = (sent[0], sent[1], sent[2].astype(jnp.float32))
        other = (received[0], received[1], received[2].astype(jnp.float32))
        is_low = (place & bit) == 0
        lo = jax.tree.map(lambda a, b: jnp.where(is_low, a, b), own, other)
        hi = jax.tree.map(lambda a, b: jnp.where(is_low, b, a), own, other)
        state = pool_combine(lo, hi)
        bit *= 2
    rows = (state[2] / state[1][:, None]).astype(jnp.bfloat16)
    bit = 1
    while bit * 2 <= count and len(gather_bits) < scatter_rounds:
        gather_bits.append(bit)
        bit *= 2
    for bit in reversed(gather_bits):
        received = xor_exchange(rows, axis, bit)
        upper = (place & bit) != 0
        rows = jnp.where(
            upper,
            jnp.concatenate([received, rows], axis=0),
            jnp.concatenate([rows, received], axis=0),
        )
    return rows


def all_to_all_pool(local, axis):
    count = lax.axis_size(axis)
    local_top, weight_sum, weighted_sum = local
    row_total, width = weighted_sum.shape
    rows = row_total // count
    stats = jnp.stack(split_wide(local_top) + split_wide(weight_sum), axis=0)
    stats = stats.reshape(4, count, rows).transpose(1, 2, 0)
    packed = jnp.concatenate(
        [
            weighted_sum.astype(jnp.bfloat16).reshape(count, rows, width),
            jnp.pad(stats, ((0, 0), (0, 0), (0, 124))),
        ],
        axis=2,
    )
    moved = lax.all_to_all(packed, axis, 0, 0, tiled=True)
    parts = moved[:, :, :width].astype(jnp.float32)
    got = moved[:, :, width : width + 4].astype(jnp.float32)
    tops = got[:, :, 0] + got[:, :, 1]
    totals = got[:, :, 2] + got[:, :, 3]
    top = jnp.max(tops, axis=0)
    scale = jnp.exp(tops - top[None, :])
    total = jnp.sum(totals * scale, axis=0)
    summed = jnp.sum(parts * scale[:, :, None], axis=0)
    finished = (summed / total[:, None]).astype(jnp.bfloat16)
    spread_rows = jnp.broadcast_to(finished[None], (count, rows, width))
    gathered = lax.all_to_all(spread_rows, axis, 0, 0, tiled=True)
    return gathered.reshape(row_total, width)


def body(
    ssm_input,
    gate_input,
    state_proj,
    step_raw,
    decay_log,
    skip_gain,
    norm_gain,
    out_weight,
    latents,
    lengths,
):
    row_count = ssm_input.shape[1]
    inner_width = ssm_input.shape[2]
    head_count = decay_log.shape[1]
    head_size = inner_width // head_count
    state_size = state_proj.shape[2] // 4
    model_width = out_weight.shape[1]
    positions = lax.axis_index("seq") * row_count + jnp.arange(row_count, dtype=jnp.int32)
    is_valid = positions < lengths[0]
    step_size = jnp.where(is_valid[None, :], jax.nn.softplus(step_raw[0]), 0.0)
    decay_rates = jnp.exp(decay_log)
    flat_tokens = ssm_input[0]
    tokens = flat_tokens.reshape(row_count, head_count, head_size)
    projections = state_proj[0]
    forward_totals, forward_records = block_pass(
        tokens,
        step_size[:head_count],
        projections[:, :state_size],
        projections[:, state_size : 2 * state_size],
        decay_rates[0],
        False,
    )
    backward_totals, backward_records = block_pass(
        tokens,
        step_size[head_count:],
        projections[:, 2 * state_size : 3 * state_size],
        projections[:, 3 * state_size :],
        decay_rates[1],
        True,
    )
    weight_groups = lax.axis_size("dp")
    full_weight = lax.all_to_all(
        jnp.broadcast_to(out_weight[None], (weight_groups,) + out_weight.shape),
        "dp",
        0,
        0,
        tiled=True,
    ).reshape(weight_groups * out_weight.shape[0], out_weight.shape[1])
    forward_in, backward_in, full_weight = transposed_scans(
        forward_totals, backward_totals, "seq", full_weight
    )
    forward_out = apply_state(forward_records, forward_in)
    backward_out = apply_state(backward_records, backward_in)
    skip_wide = jnp.repeat(skip_gain, head_size)
    mixed_out = forward_out + backward_out + skip_wide[None, :] * flat_tokens.astype(jnp.float32)
    gated_out = mixed_out * jax.nn.silu(gate_input[0].astype(jnp.float32))
    squared = (gated_out * gated_out).reshape(row_count, head_count, head_size)
    mean_square = jnp.mean(squared, axis=2)
    inverse_scale = jnp.repeat(lax.rsqrt(mean_square + 1e-05), head_size, axis=1)
    normed = (gated_out * inverse_scale * norm_gain[None, :]).astype(jnp.bfloat16)
    projected = jnp.dot(normed, full_weight, preferred_element_type=jnp.float32)
    encoded = projected.astype(jnp.bfloat16)
    score_scale = 1.0 / math.sqrt(model_width)
    scores = (
        jnp.einsum("rd,sd->rs", latents, encoded, preferred_element_type=jnp.float32) * score_scale
    )
    local_top = jnp.max(jnp.where(is_valid[None, :], scores, -1e30), axis=1)
    prob_values = jnp.where(is_valid[None, :], jnp.exp(scores - local_top[:, None]), 0.0)
    weight_sum = jnp.sum(prob_values, axis=1)
    weighted_sum = jnp.dot(
        prob_values.astype(jnp.bfloat16), encoded, preferred_element_type=jnp.float32
    )
    pooled = all_to_all_pool((local_top, weight_sum, weighted_sum), "seq")
    return (encoded[None], pooled[None])


def solution(mesh):
    in_specs = (
        P("dp", "seq", None),
        P("dp", "seq", None),
        P("dp", "seq", None),
        P("dp", None, "seq"),
        P(),
        P(),
        P(),
        P("dp", None),
        P(),
        P("dp"),
    )
    out_specs = (P("dp", "seq", None), P("dp", None, None))
    return jax.shard_map(body, mesh=mesh, in_specs=in_specs, out_specs=out_specs, check_vma=False)
```
